128 devices in a mesh: ctx: 32 (over z, y, x_hi), mp: 4 (over x_lo, core).
Axes of the slice: x: 4 (x_hi: 2, x_lo: 2; x = x_hi * 2 + x_lo), y: 4, z: 4, core: 2. Of those that a mesh axis runs over, the one named last changes fastest.
Arguments:
- queries: bfloat16 [2, 6144, 5120], P(None, 'ctx', 'mp'), may hold values from -24 to 24
- cache_keys: bfloat16 [6144, 5120], P(('ctx', 'mp')), may hold values from -26 to 26
- cache_values: bfloat16 [6144, 5120], P(('ctx', 'mp')), may hold values from -6 to 6
- douts: bfloat16 [2, 6144, 5120], P(None, 'ctx', 'mp'), may hold values from -6 to 6
- reads: int32 [32, 96], P('ctx'), may hold values from -1 to 383, as said below
Outputs:
- attn_out: bfloat16 [2, 6144, 5120], P(None, 'ctx', 'mp')
- d_queries: bfloat16 [2, 6144, 5120], P(None, 'ctx', 'mp')
- d_cache_keys: float32 [6144, 5120], P(('ctx', 'mp'))
- d_cache_values: float32 [6144, 5120], P(('ctx', 'mp'))
The draws below stay inside these ranges and needn't reach their ends.
Inputs may be any that keep to these rules, and one draw needn't show every extreme that they name: Row c names, in rising order, the blocks that stretch c reads, then -1 in the remaining slots. Every named block ends at or before stretch c's last position. Block 0 is named in every row. Owner o holds blocks 3 * o to 3 * o + 2; a row names at most one block of an owner, and exactly one of each of the 4 owners of stretch c's own positions. Row c names min(96, 4 * (c + 1)) blocks.
All inputs are finite; a program needn't handle non-finite values.
Results may differ from the reference program's by a relative error of at most 0.017.
Values may be sent and summed in bfloat16 or wider, within the bound.
No kernel may reach another device: no remote copies, remote signals or barrier semaphores. Data moves between devices by JAX's collectives and lax.ppermute only.
A program may use at most 256 MiB of HBM per device.

```python
import math
import jax
import jax.numpy as jnp
from jax import lax

HEADS = 40
HD = 128
LAYERS = 2
BLK = 16
TOK_DEV = 192
STRETCHES = 32
OWNERS = 128
SEQ = 6144
BPD = 3
READS = 96
N_MP = 4


def chosen_reads(key):
    folded = jax.random.fold_in(key, 101)
    key_rank, key_block = jax.random.split(folded)
    owners = jnp.arange(OWNERS, dtype=jnp.int32)
    stretches = jnp.arange(STRETCHES, dtype=jnp.int32)[:, None]
    home_stretch = owners[None, :] // N_MP
    forced = (home_stretch == stretches) | (owners[None, :] == 0)
    reach = home_stretch <= stretches
    rank_noise = jax.random.randint(key_rank, (STRETCHES, OWNERS), 0, 1 << 16) * OWNERS + owners[None, :]
    beyond_score = (1 << 16) * OWNERS + owners[None, :]
    rank_score = jnp.where(forced, owners[None, :] - OWNERS, jnp.where(reach, rank_noise, beyond_score))
    owner_rank = jnp.argsort(jnp.argsort(rank_score, axis=1), axis=1)
    read_count = jnp.minimum(READS, N_MP * (stretches + 1))
    picked = owner_rank < read_count
    local_block = jax.random.randint(key_block, (STRETCHES, OWNERS), 0, BPD)
    local_block = jnp.where(owners[None, :] == 0, 0, local_block)
    block_ids = owners[None, :] * BPD + local_block
    beyond = OWNERS * BPD
    listed = jnp.sort(jnp.where(picked, block_ids, beyond), axis=1)[:, :READS]
    return jnp.where(listed == beyond, -1, listed).astype(jnp.int32)


def draw_reads(key, part):
    listed = chosen_reads(key)
    return listed


def draw_cache_keys(key, part):
    drawn = jax.random.normal(jax.random.fold_in(key, 109), (SEQ, HEADS * HD), jnp.float32)
    drawn = jnp.clip(drawn, -6.0, 6.0)
    return drawn.astype(jnp.bfloat16)


def draw_queries(key, part):
    drawn = jax.random.normal(jax.random.fold_in(key, 127), (LAYERS, SEQ, HEADS * HD), jnp.float32)
    drawn = jnp.clip(drawn, -6.0, 6.0)
    return drawn.astype(jnp.bfloat16)


def shard_levels(key, shape, cuts, low, largest):
    gain = 1.0
    for dim, shards_of in cuts:
        steps = jax.random.uniform(jax.random.fold_in(jax.random.fold_in(key, 6), dim), (shards_of,), jnp.float32, low / len(cuts), largest / len(cuts))
        gain = gain * jnp.repeat(jnp.exp(steps), shape[dim] // shards_of).reshape((-1,) + (1,) * (len(shape) - 1 - dim))
    return gain


def noise(own_key, extent, spread, most, shards=(), held_as=jnp.bfloat16):
    values = jax.random.normal(own_key, extent, jnp.float32) * spread
    if len(shards) > 0:
        values = shard_levels(own_key, extent, shards, -0.22, 0.18) * values
    return jnp.clip(values, min=-most, max=most).astype(held_as)


def setup_inputs(seed: int = 0) -> dict:
    splits = jax.random.split(jax.random.key(seed), 6)
    return {
        "queries": draw_queries(jax.random.fold_in(splits[5], 71), 0),
        "cache_keys": draw_cache_keys(jax.random.fold_in(splits[5], 71), 0),
        "cache_values": noise(splits[2], (SEQ, HEADS * HD), 1.0, 6.0, ((0, 128),)),
        "douts": noise(splits[3], (LAYERS, SEQ, HEADS * HD), 1.0, 6.0, ((1, 32), (2, 4))),
        "reads": draw_reads(jax.random.fold_in(splits[5], 71), 0),
    }


neg_big = -1e+30

def reference(queries, cache_keys, cache_values, douts, reads):
    factor = 1.0 / math.sqrt(HD)
    offsets = jnp.arange(BLK, dtype=jnp.int32)
    rows_here = jnp.arange(TOK_DEV, dtype=jnp.int32)

    def one_stretch(running, stretch_id):
        grad_keys, grad_values = running
        listed = lax.dynamic_index_in_dim(reads, stretch_id, 0, keepdims=False)
        in_use = listed >= 0
        clamped = jnp.where(in_use, listed, 0).astype(jnp.int32)
        key_pos = (clamped[:, None] * BLK + offsets[None, :]).reshape(-1).astype(jnp.int32)
        key_live = jnp.repeat(in_use, BLK)
        query_pos = stretch_id * TOK_DEV + rows_here
        visible = key_live[None, :] & (key_pos[None, :] <= query_pos[:, None])
        key_rows = cache_keys[key_pos].astype(jnp.float32).reshape(-1, HEADS, HD)
        value_rows = cache_values[key_pos].astype(jnp.float32).reshape(-1, HEADS, HD)
        key_sum = jnp.zeros(key_rows.shape, jnp.float32)
        value_sum = jnp.zeros(value_rows.shape, jnp.float32)
        outs_here = []
        grads_here = []
        for layer_id in range(LAYERS):
            query_rows = lax.dynamic_slice_in_dim(queries[layer_id], stretch_id * TOK_DEV, TOK_DEV, 0)
            query_rows = query_rows.astype(jnp.float32).reshape(TOK_DEV, HEADS, HD)
            dout_rows = lax.dynamic_slice_in_dim(douts[layer_id], stretch_id * TOK_DEV, TOK_DEV, 0)
            dout_rows = dout_rows.astype(jnp.float32).reshape(TOK_DEV, HEADS, HD)
            scores = jnp.einsum('qhd,khd->hqk', query_rows, key_rows) * factor
            scores = jnp.where(visible[None], scores, neg_big)
            row_top = lax.optimization_barrier(jnp.max(scores, axis=2, keepdims=True))
            raised = jnp.exp(scores - row_top)
            prob_full = raised / lax.optimization_barrier(jnp.sum(raised, axis=2, keepdims=True))
            probs_low = lax.optimization_barrier(prob_full.astype(jnp.bfloat16)).astype(jnp.float32)
            attended = jnp.einsum('hqk,khd->qhd', probs_low, value_rows).astype(jnp.bfloat16)
            row_delta = lax.optimization_barrier(jnp.sum(dout_rows * attended.astype(jnp.float32), axis=2))
            d_probs = jnp.einsum('qhd,khd->hqk', dout_rows, value_rows)
            d_scores = prob_full * (d_probs - row_delta.T[:, :, None])
            d_scores = lax.optimization_barrier(d_scores.astype(jnp.bfloat16)).astype(jnp.float32)
            d_query = (jnp.einsum('hqk,khd->qhd', d_scores, key_rows) * factor).astype(jnp.bfloat16)
            key_sum = key_sum + jnp.einsum('hqk,qhd->khd', d_scores, query_rows) * factor
            value_sum = value_sum + jnp.einsum('hqk,qhd->khd', probs_low, dout_rows)
            outs_here.append(attended.reshape(TOK_DEV, HEADS * HD))
            grads_here.append(d_query.reshape(TOK_DEV, HEADS * HD))
        grad_keys = grad_keys.at[key_pos].add(key_sum.reshape(-1, HEADS * HD))
        grad_values = grad_values.at[key_pos].add(value_sum.reshape(-1, HEADS * HD))
        return ((grad_keys, grad_values), (jnp.stack(outs_here), jnp.stack(grads_here)))
    start = (jnp.zeros((SEQ, HEADS * HD), jnp.float32), jnp.zeros((SEQ, HEADS * HD), jnp.float32))
    finals, stacked = lax.scan(one_stretch, start, jnp.arange(STRETCHES, dtype=jnp.int32))
    attn_out = stacked[0].transpose(1, 0, 2, 3).reshape(LAYERS, SEQ, HEADS * HD)
    d_queries = stacked[1].transpose(1, 0, 2, 3).reshape(LAYERS, SEQ, HEADS * HD)
    return (attn_out, d_queries, finals[0], finals[1])
```

```python
import functools
import math

import jax
import jax.numpy as jnp
from jax import lax
from jax.experimental import pallas as pl
from jax.experimental.pallas import tpu as pltpu
from jax.sharding import PartitionSpec as P

HD = 128
BLK = 16

neg_big = -1e30
far_pos = 1 << 30


def fetch_blocks(operands):
    return (
        lax.all_to_all(operands[0], ("ctx", "mp"), split_axis=0, concat_axis=0, tiled=True),
        lax.all_to_all(operands[1], ("ctx", "mp"), split_axis=0, concat_axis=0, tiled=True),
    )


def return_grads(operands):
    return (
        lax.all_to_all(operands[0], ("ctx", "mp"), split_axis=0, concat_axis=0, tiled=True),
        lax.all_to_all(operands[1], ("ctx", "mp"), split_axis=0, concat_axis=0, tiled=True),
    )


def attend_kernel(
    kpos_ref, q_ref, do_ref, k_ref, v_ref, o_ref, dq_ref, dk_ref, dv_ref, dk_acc, dv_acc,
    *, factor, layer_count
):
    layer_id = pl.program_id(1)
    q = q_ref[0]
    do = do_ref[0]
    k = k_ref[...]
    v = v_ref[...]
    tok_rows = q.shape[0]
    rows = lax.broadcasted_iota(jnp.int32, (tok_rows, 1), 0)
    visible = kpos_ref[...] <= rows
    scores = lax.dot_general(
        q, k, (((1,), (1,)), ((), ())), preferred_element_type=jnp.float32
    ) * factor
    scores = jnp.where(visible, scores, neg_big)
    row_top = jnp.max(scores, axis=1, keepdims=True)
    raised = jnp.exp(scores - row_top)
    row_total = jnp.sum(raised, axis=1, keepdims=True)
    probs = raised * (1.0 / row_total)
    probs_low = probs.astype(jnp.bfloat16)
    attended = jnp.dot(probs_low, v, preferred_element_type=jnp.float32).astype(jnp.bfloat16)
    o_ref[0] = attended
    row_delta = jnp.sum(
        do.astype(jnp.float32) * attended.astype(jnp.float32), axis=1, keepdims=True
    )
    d_probs = lax.dot_general(
        do, v, (((1,), (1,)), ((), ())), preferred_element_type=jnp.float32
    )
    d_scores = (probs * (d_probs - row_delta)).astype(jnp.bfloat16)
    dq = jnp.dot(d_scores, k, preferred_element_type=jnp.float32) * factor
    dq_ref[0] = dq.astype(jnp.bfloat16)
    dk = lax.dot_general(
        d_scores, q, (((0,), (0,)), ((), ())), preferred_element_type=jnp.float32
    ) * factor
    dv = lax.dot_general(
        probs_low, do, (((0,), (0,)), ((), ())), preferred_element_type=jnp.float32
    )

    @pl.when(layer_id == 0)
    def _():
        dk_acc[...] = dk
        dv_acc[...] = dv

    @pl.when(layer_id > 0)
    def _():
        dk_acc[...] += dk
        dv_acc[...] += dv

    @pl.when(layer_id == layer_count - 1)
    def _():
        dk_ref[...] = dk_acc[...].astype(jnp.bfloat16)
        dv_ref[...] = dv_acc[...].astype(jnp.bfloat16)


def attend(kpos_rel, queries, douts, key_rows, value_rows, factor):
    layer_count, tok_rows, head_width = queries.shape
    key_total = key_rows.shape[0]
    head_count = head_width // HD
    kernel = functools.partial(attend_kernel, factor=factor, layer_count=layer_count)
    tok_spec = pl.BlockSpec((1, tok_rows, HD), lambda h, l: (l, 0, h))
    key_spec = pl.BlockSpec((key_total, HD), lambda h, l: (0, h))
    return pl.pallas_call(
        kernel,
        grid=(head_count, layer_count),
        in_specs=[
            pl.BlockSpec((1, key_total), lambda h, l: (0, 0)),
            tok_spec,
            tok_spec,
            key_spec,
            key_spec,
        ],
        out_specs=[tok_spec, tok_spec, key_spec, key_spec],
        out_shape=[
            jax.ShapeDtypeStruct(queries.shape, jnp.bfloat16),
            jax.ShapeDtypeStruct(queries.shape, jnp.bfloat16),
            jax.ShapeDtypeStruct(key_rows.shape, jnp.bfloat16),
            jax.ShapeDtypeStruct(key_rows.shape, jnp.bfloat16),
        ],
        scratch_shapes=[
            pltpu.VMEM((key_total, HD), jnp.float32),
            pltpu.VMEM((key_total, HD), jnp.float32),
        ],
        compiler_params=pltpu.CompilerParams(
            dimension_semantics=("arbitrary", "arbitrary"),
            vmem_limit_bytes=48 * 1024 * 1024,
        ),
    )(kpos_rel, queries, douts, key_rows, value_rows)


def on_device(queries, cache_keys, cache_values, douts, reads):
    layer_count, tok_rows, head_width = queries.shape
    kv_rows, full_width = cache_keys.shape
    ctx_count = lax.axis_size("ctx")
    mp_count = lax.axis_size("mp")
    owner_count = ctx_count * mp_count
    per_owner = kv_rows // BLK
    my_owner = lax.axis_index(("ctx", "mp"))
    my_stretch = lax.axis_index("ctx")
    my_mp = lax.axis_index("mp")
    factor = 1.0 / math.sqrt(HD)
    placed = jnp.where(
        (jnp.arange(ctx_count, dtype=jnp.int32) == my_stretch)[:, None] & (my_mp == 0),
        reads,
        0,
    )
    all_lists = lax.psum(placed, ("ctx", "mp"))
    owner_hit = (all_lists >= 0) & (all_lists // per_owner == my_owner)
    chosen = jnp.sum(jnp.where(owner_hit, all_lists - my_owner * per_owner, 0), axis=1)
    wanted = jnp.any(owner_hit, axis=1)
    picker = (chosen[:, None] == jnp.arange(per_owner, dtype=jnp.int32)[None, :]) & wanted[:, None]
    picker_low = picker.astype(jnp.bfloat16)
    picker_full = picker.astype(jnp.float32)

    def outgoing(cache_rows):
        block_grid = cache_rows.reshape(per_owner, BLK * full_width)
        picked = jnp.dot(picker_low, block_grid, preferred_element_type=jnp.float32).astype(
            jnp.bfloat16
        )
        picked = picked.reshape(ctx_count, BLK, mp_count, head_width).transpose(0, 2, 1, 3)
        return picked.reshape(owner_count, BLK, head_width)

    def absorb(returned):
        block_grid = returned.reshape(ctx_count, mp_count, BLK, head_width).transpose(0, 2, 1, 3)
        block_grid = block_grid.reshape(ctx_count, BLK * full_width)
        summed = jnp.dot(
            picker_full.T,
            block_grid.astype(jnp.float32),
            precision=lax.Precision.HIGHEST,
            preferred_element_type=jnp.float32,
        )
        return summed.reshape(kv_rows, full_width)

    own_list = reads[0]
    owner_ids = jnp.arange(owner_count, dtype=jnp.int32)
    slot_hit = (own_list[:, None] >= 0) & (own_list[:, None] // per_owner == owner_ids[None, :])
    slot_live = jnp.any(slot_hit, axis=0)
    slot_block = jnp.sum(
        jnp.where(slot_hit, own_list[:, None] - owner_ids[None, :] * per_owner, 0), axis=0
    )
    slot_start = owner_ids * kv_rows + slot_block * BLK
    key_pos = (slot_start[:, None] + jnp.arange(BLK, dtype=jnp.int32)[None, :]).reshape(-1)
    key_live = jnp.repeat(slot_live, BLK)
    kpos_rel = jnp.where(key_live, key_pos - my_stretch * tok_rows, far_pos)
    kpos_rel = kpos_rel.reshape(1, -1).astype(jnp.int32)
    slot_shape = (owner_count, BLK, head_width)
    got_keys, got_values = fetch_blocks((outgoing(cache_keys), outgoing(cache_values)))
    key_rows = got_keys.reshape(owner_count * BLK, head_width)
    value_rows = got_values.reshape(owner_count * BLK, head_width)
    attended, d_query, key_grads, value_grads = attend(
        kpos_rel, queries, douts, key_rows, value_rows, factor
    )
    sending = (key_grads.reshape(slot_shape), value_grads.reshape(slot_shape))
    back_keys, back_values = return_grads(sending)
    return (attended, d_query, absorb(back_keys), absorb(back_values))


def solution(mesh):
    return jax.shard_map(
        on_device,
        mesh=mesh,
        in_specs=(
            P(None, "ctx", "mp"),
            P(("ctx", "mp"), None),
            P(("ctx", "mp"), None),
            P(None, "ctx", "mp"),
            P("ctx", None),
        ),
        out_specs=(
            P(None, "ctx", "mp"),
            P(None, "ctx", "mp"),
            P(("ctx", "mp"), None),
            P(("ctx", "mp"), None),
        ),
        check_vma=False,
    )
```

```python
import functools
import math

import jax
import jax.numpy as jnp
from jax import lax
from jax.experimental import pallas as pl
from jax.experimental.pallas import tpu as pltpu
from jax.sharding import PartitionSpec as P

HD = 128
BLK = 16

neg_big = -1e30
far_pos = 1 << 30


def exchange(operand):
    return lax.all_to_all(operand, ("ctx", "mp"), split_axis=0, concat_axis=0, tiled=True)


def attend_kernel(
    kpos_ref, q_ref, do_ref, kv_ref, o_ref, dq_ref, dkv_ref, dk_acc, dv_acc,
    *, factor, layer_count
):
    layer_id = pl.program_id(1)
    q = q_ref[0]
    do = do_ref[0]
    key_total = dk_acc.shape[0]
    k = kv_ref[:, 0].reshape(key_total, HD)
    v = kv_ref[:, 1].reshape(key_total, HD)
    tok_rows = q.shape[0]
    rows = lax.broadcasted_iota(jnp.int32, (tok_rows, 1), 0)
    visible = kpos_ref[...] <= rows
    scores = lax.dot_general(
        q, k, (((1,), (1,)), ((), ())), preferred_element_type=jnp.float32
    ) * factor
    scores = jnp.where(visible, scores, neg_big)
    row_top = jnp.max(scores, axis=1, keepdims=True)
    raised = jnp.exp(scores - row_top)
    row_total = jnp.sum(raised, axis=1, keepdims=True)
    probs = raised * (1.0 / row_total)
    probs_low = probs.astype(jnp.bfloat16)
    attended = jnp.dot(probs_low, v, preferred_element_type=jnp.float32).astype(jnp.bfloat16)
    o_ref[0] = attended
    row_delta = jnp.sum(
        do.astype(jnp.float32) * attended.astype(jnp.float32), axis=1, keepdims=True
    )
    d_probs = lax.dot_general(
        do, v, (((1,), (1,)), ((), ())), preferred_element_type=jnp.float32
    )
    d_scores = (probs * (d_probs - row_delta)).astype(jnp.bfloat16)
    dq = jnp.dot(d_scores, k, preferred_element_type=jnp.float32) * factor
    dq_ref[0] = dq.astype(jnp.bfloat16)
    dk = lax.dot_general(
        d_scores, q, (((0,), (0,)), ((), ())), preferred_element_type=jnp.float32
    ) * factor
    dv = lax.dot_general(
        probs_low, do, (((0,), (0,)), ((), ())), preferred_element_type=jnp.float32
    )

    @pl.when(layer_id == 0)
    def _():
        dk_acc[...] = dk
        dv_acc[...] = dv

    @pl.when(layer_id > 0)
    def _():
        dk_acc[...] += dk
        dv_acc[...] += dv

    @pl.when(layer_id == layer_count - 1)
    def _():
        dkv_ref[:, 0] = dk_acc[...].astype(jnp.bfloat16).reshape(dkv_ref.shape[0], BLK, HD)
        dkv_ref[:, 1] = dv_acc[...].astype(jnp.bfloat16).reshape(dkv_ref.shape[0], BLK, HD)


def attend(kpos_rel, queries, douts, kv_rows, factor):
    layer_count, tok_rows, head_width = queries.shape
    slot_count = kv_rows.shape[0]
    key_total = slot_count * BLK
    head_count = head_width // HD
    kernel = functools.partial(attend_kernel, factor=factor, layer_count=layer_count)
    tok_spec = pl.BlockSpec((1, tok_rows, HD), lambda h, l: (l, 0, h))
    kv_spec = pl.BlockSpec((slot_count, 2, BLK, HD), lambda h, l: (0, 0, 0, h))
    return pl.pallas_call(
        kernel,
        grid=(head_count, layer_count),
        in_specs=[
            pl.BlockSpec((1, key_total), lambda h, l: (0, 0)),
            tok_spec,
            tok_spec,
            kv_spec,
        ],
        out_specs=[tok_spec, tok_spec, kv_spec],
        out_shape=[
            jax.ShapeDtypeStruct(queries.shape, jnp.bfloat16),
            jax.ShapeDtypeStruct(queries.shape, jnp.bfloat16),
            jax.ShapeDtypeStruct(kv_rows.shape, jnp.bfloat16),
        ],
        scratch_shapes=[
            pltpu.VMEM((key_total, HD), jnp.float32),
            pltpu.VMEM((key_total, HD), jnp.float32),
        ],
        compiler_params=pltpu.CompilerParams(
            dimension_semantics=("arbitrary", "arbitrary"),
            vmem_limit_bytes=48 * 1024 * 1024,
        ),
    )(kpos_rel, queries, douts, kv_rows)


def on_device(queries, cache_keys, cache_values, douts, reads):
    layer_count, tok_rows, head_width = queries.shape
    kv_rows, full_width = cache_keys.shape
    ctx_count = lax.axis_size("ctx")
    mp_count = lax.axis_size("mp")
    owner_count = ctx_count * mp_count
    per_owner = kv_rows // BLK
    my_owner = lax.axis_index(("ctx", "mp"))
    my_stretch = lax.axis_index("ctx")
    my_mp = lax.axis_index("mp")
    factor = 1.0 / math.sqrt(HD)
    spread = jnp.broadcast_to(reads, (owner_count, reads.shape[1]))
    all_lists = exchange(spread).reshape(ctx_count, mp_count, -1)[:, 0, :]
    owner_hit = (all_lists >= 0) & (all_lists // per_owner == my_owner)
    chosen = jnp.sum(jnp.where(owner_hit, all_lists - my_owner * per_owner, 0), axis=1)
    wanted = jnp.any(owner_hit, axis=1)
    picker = (chosen[:, None] == jnp.arange(per_owner, dtype=jnp.int32)[None, :]) & wanted[:, None]
    picker_low = picker.astype(jnp.bfloat16)

    def by_block(cache_rows):
        return cache_rows.reshape(per_owner, BLK, mp_count, head_width).transpose(0, 2, 1, 3)

    def outgoing():
        block_grid = jnp.stack([by_block(cache_keys), by_block(cache_values)], axis=2)
        block_grid = block_grid.reshape(per_owner, mp_count * 2 * BLK * head_width)
        picked = jnp.dot(picker_low, block_grid, preferred_element_type=jnp.float32)
        return picked.astype(jnp.bfloat16).reshape(owner_count, 2, BLK, head_width)

    def absorb(returned):
        block_grid = returned.reshape(ctx_count, mp_count * 2 * BLK * head_width)
        summed = jnp.dot(picker_low.T, block_grid, preferred_element_type=jnp.float32)
        summed = summed.reshape(per_owner, mp_count, 2, BLK, head_width).transpose(2, 0, 3, 1, 4)
        summed = summed.reshape(2, kv_rows, full_width)
        return summed[0], summed[1]

    own_list = reads[0]
    owner_ids = jnp.arange(owner_count, dtype=jnp.int32)
    slot_hit = (own_list[:, None] >= 0) & (own_list[:, None] // per_owner == owner_ids[None, :])
    slot_live = jnp.any(slot_hit, axis=0)
    slot_block = jnp.sum(
        jnp.where(slot_hit, own_list[:, None] - owner_ids[None, :] * per_owner, 0), axis=0
    )
    slot_start = owner_ids * kv_rows + slot_block * BLK
    key_pos = (slot_start[:, None] + jnp.arange(BLK, dtype=jnp.int32)[None, :]).reshape(-1)
    key_live = jnp.repeat(slot_live, BLK)
    kpos_rel = jnp.where(key_live, key_pos - my_stretch * tok_rows, far_pos)
    kpos_rel = kpos_rel.reshape(1, -1).astype(jnp.int32)
    kv_rows_got = exchange(outgoing())
    attended, d_query, kv_grads = attend(kpos_rel, queries, douts, kv_rows_got, factor)
    grad_keys, grad_values = absorb(exchange(kv_grads))
    return (attended, d_query, grad_keys, grad_values)


def solution(mesh):
    return jax.shard_map(
        on_device,
        mesh=mesh,
        in_specs=(
            P(None, "ctx", "mp"),
            P(("ctx", "mp"), None),
            P(("ctx", "mp"), None),
            P(None, "ctx", "mp"),
            P("ctx", None),
        ),
        out_specs=(
            P(None, "ctx", "mp"),
            P(None, "ctx", "mp"),
            P(("ctx", "mp"), None),
            P(("ctx", "mp"), None),
        ),
        check_vma=False,
    )
```

```python
import functools
import math

import jax
import jax.numpy as jnp
from jax import lax
from jax.experimental import pallas as pl
from jax.experimental.pallas import tpu as pltpu
from jax.sharding import PartitionSpec as P

HD = 128
BLK = 16

neg_big = -1e30
far_pos = 1 << 30


def exchange(operand):
    return lax.all_to_all(operand, ("ctx", "mp"), split_axis=0, concat_axis=0, tiled=True)


def attend_kernel(
    kpos_ref, q_ref, do_ref, kv_ref, o_ref, dq_ref, dkv_ref, dk_acc, dv_acc,
    *, factor, layer_count
):
    layer_id = pl.program_id(1)
    q = q_ref[0]
    do = do_ref[0]
    key_total = dk_acc.shape[0]
    k = kv_ref[:, 0].reshape(key_total, HD)
    v = kv_ref[:, 1].reshape(key_total, HD)
    tok_rows = q.shape[0]
    rows = lax.broadcasted_iota(jnp.int32, (tok_rows, 1), 0)
    visible = kpos_ref[...] <= rows
    scores = lax.dot_general(
        q, k, (((1,), (1,)), ((), ())), preferred_element_type=jnp.float32
    ) * factor
    scores = jnp.where(visible, scores, neg_big)
    row_top = jnp.max(scores, axis=1, keepdims=True)
    raised = jnp.exp(scores - row_top)
    row_total = jnp.sum(raised, axis=1, keepdims=True)
    probs = raised * (1.0 / row_total)
    probs_low = probs.astype(jnp.bfloat16)
    attended = jnp.dot(probs_low, v, preferred_element_type=jnp.float32).astype(jnp.bfloat16)
    o_ref[0] = attended
    row_delta = jnp.sum(
        do.astype(jnp.float32) * attended.astype(jnp.float32), axis=1, keepdims=True
    )
    d_probs = lax.dot_general(
        do, v, (((1,), (1,)), ((), ())), preferred_element_type=jnp.float32
    )
    d_scores = (probs * (d_probs - row_delta)).astype(jnp.bfloat16)
    dq = jnp.dot(d_scores, k, preferred_element_type=jnp.float32) * factor
    dq_ref[0] = dq.astype(jnp.bfloat16)
    dk = lax.dot_general(
        d_scores, q, (((0,), (0,)), ((), ())), preferred_element_type=jnp.float32
    ) * factor
    dv = lax.dot_general(
        probs_low, do, (((0,), (0,)), ((), ())), preferred_element_type=jnp.float32
    )

    @pl.when(layer_id == 0)
    def _():
        dk_acc[...] = dk
        dv_acc[...] = dv

    @pl.when(layer_id > 0)
    def _():
        dk_acc[...] += dk
        dv_acc[...] += dv

    @pl.when(layer_id == layer_count - 1)
    def _():
        dkv_ref[:, 0] = dk_acc[...].astype(jnp.bfloat16).reshape(dkv_ref.shape[0], BLK, HD)
        dkv_ref[:, 1] = dv_acc[...].astype(jnp.bfloat16).reshape(dkv_ref.shape[0], BLK, HD)


def attend(kpos_rel, queries, douts, kv_rows, factor):
    layer_count, tok_rows, head_width = queries.shape
    slot_count = kv_rows.shape[0]
    key_total = slot_count * BLK
    head_count = head_width // HD
    kernel = functools.partial(attend_kernel, factor=factor, layer_count=layer_count)
    tok_spec = pl.BlockSpec((1, tok_rows, HD), lambda h, l: (l, 0, h))
    kv_spec = pl.BlockSpec((slot_count, 2, BLK, HD), lambda h, l: (0, 0, 0, h))
    return pl.pallas_call(
        kernel,
        grid=(head_count, layer_count),
        in_specs=[
            pl.BlockSpec((1, key_total), lambda h, l: (0, 0)),
            tok_spec,
            tok_spec,
            kv_spec,
        ],
        out_specs=[tok_spec, tok_spec, kv_spec],
        out_shape=[
            jax.ShapeDtypeStruct(queries.shape, jnp.bfloat16),
            jax.ShapeDtypeStruct(queries.shape, jnp.bfloat16),
            jax.ShapeDtypeStruct(kv_rows.shape, jnp.bfloat16),
        ],
        scratch_shapes=[
            pltpu.VMEM((key_total, HD), jnp.float32),
            pltpu.VMEM((key_total, HD), jnp.float32),
        ],
        compiler_params=pltpu.CompilerParams(
            dimension_semantics=("arbitrary", "arbitrary"),
            vmem_limit_bytes=48 * 1024 * 1024,
        ),
    )(kpos_rel, queries, douts, kv_rows)


def on_device(queries, cache_keys, cache_values, douts, reads):
    layer_count, tok_rows, head_width = queries.shape
    kv_rows, full_width = cache_keys.shape
    ctx_count = lax.axis_size("ctx")
    mp_count = lax.axis_size("mp")
    owner_count = ctx_count * mp_count
    per_owner = kv_rows // BLK
    my_owner = lax.axis_index(("ctx", "mp"))
    my_stretch = lax.axis_index("ctx")
    my_mp = lax.axis_index("mp")
    factor = 1.0 / math.sqrt(HD)
    spread = jnp.broadcast_to(reads, (owner_count, reads.shape[1]))
    all_lists = exchange(spread).reshape(ctx_count, mp_count, -1)[:, 0, :]
    owner_hit = (all_lists >= 0) & (all_lists // per_owner == my_owner)
    chosen = jnp.sum(jnp.where(owner_hit, all_lists - my_owner * per_owner, 0), axis=1)
    wanted = jnp.any(owner_hit, axis=1)
    picker = (chosen[:, None] == jnp.arange(per_owner, dtype=jnp.int32)[None, :]) & wanted[:, None]
    picker_low = picker.astype(jnp.bfloat16)

    def by_block(cache_rows):
        return cache_rows.reshape(per_owner, BLK, mp_count, head_width).transpose(0, 2, 1, 3)

    def outgoing():
        block_grid = jnp.stack([by_block(cache_keys), by_block(cache_values)], axis=2)
        picked = jnp.zeros((ctx_count,) + block_grid.shape[1:], jnp.bfloat16)
        for block_id in range(per_owner):
            hit = picker[:, block_id].reshape(ctx_count, 1, 1, 1, 1)
            picked = jnp.where(hit, block_grid[block_id][None], picked)
        return picked.reshape(owner_count, 2, BLK, head_width)

    def absorb(returned):
        block_grid = returned.reshape(ctx_count, mp_count, 2, BLK, head_width)
        summed = lax.dot_general(
            picker_low, block_grid, (((0,), (0,)), ((), ())), preferred_element_type=jnp.float32
        )
        summed = summed.transpose(2, 0, 3, 1, 4).reshape(2, kv_rows, full_width)
        return summed[0], summed[1]

    own_list = reads[0]
    owner_ids = jnp.arange(owner_count, dtype=jnp.int32)
    slot_hit = (own_list[:, None] >= 0) & (own_list[:, None] // per_owner == owner_ids[None, :])
    slot_live = jnp.any(slot_hit, axis=0)
    slot_block = jnp.sum(
        jnp.where(slot_hit, own_list[:, None] - owner_ids[None, :] * per_owner, 0), axis=0
    )
    slot_start = owner_ids * kv_rows + slot_block * BLK
    key_pos = (slot_start[:, None] + jnp.arange(BLK, dtype=jnp.int32)[None, :]).reshape(-1)
    key_live = jnp.repeat(slot_live, BLK)
    kpos_rel = jnp.where(key_live, key_pos - my_stretch * tok_rows, far_pos)
    kpos_rel = kpos_rel.reshape(1, -1).astype(jnp.int32)
    kv_rows_got = exchange(outgoing())
    attended, d_query, kv_grads = attend(kpos_rel, queries, douts, kv_rows_got, factor)
    grad_keys, grad_values = absorb(exchange(kv_grads))
    return (attended, d_query, grad_keys, grad_values)


def solution(mesh):
    return jax.shard_map(
        on_device,
        mesh=mesh,
        in_specs=(
            P(None, "ctx", "mp"),
            P(("ctx", "mp"), None),
            P(("ctx", "mp"), None),
            P(None, "ctx", "mp"),
            P("ctx", None),
        ),
        out_specs=(
            P(None, "ctx", "mp"),
            P(None, "ctx", "mp"),
            P(("ctx", "mp"), None),
            P(("ctx", "mp"), None),
        ),
        check_vma=False,
    )
```

```python
import functools
import math

import jax
import jax.numpy as jnp
from jax import lax
from jax.experimental import pallas as pl
from jax.experimental.pallas import tpu as pltpu
from jax.sharding import PartitionSpec as P

HD = 128
BLK = 16

neg_big = -1e30
far_pos = 1 << 30


def exchange(operand):
    return lax.all_to_all(operand, ("ctx", "mp"), split_axis=0, concat_axis=0, tiled=True)


def attend_kernel(
    kpos_ref, q_ref, do_ref, kv_ref, o_ref, dq_ref, dkv_ref, dk_acc, dv_acc,
    *, factor, layer_count
):
    layer_id = pl.program_id(1)
    q = q_ref[0]
    do = do_ref[0]
    key_total = dk_acc.shape[0]
    k = kv_ref[:, 0].reshape(key_total, HD)
    v = kv_ref[:, 1].reshape(key_total, HD)
    tok_rows = q.shape[0]
    rows = lax.broadcasted_iota(jnp.int32, (tok_rows, 1), 0)
    visible = kpos_ref[...] <= rows
    scores = lax.dot_general(
        q, k, (((1,), (1,)), ((), ())), preferred_element_type=jnp.float32
    ) * factor
    scores = jnp.where(visible, scores, neg_big)
    row_top = jnp.max(scores, axis=1, keepdims=True)
    raised = jnp.exp(scores - row_top)
    row_total = jnp.sum(raised, axis=1, keepdims=True)
    probs = raised * (1.0 / row_total)
    probs_low = probs.astype(jnp.bfloat16)
    attended = jnp.dot(probs_low, v, preferred_element_type=jnp.float32).astype(jnp.bfloat16)
    o_ref[0] = attended
    row_delta = jnp.sum(
        do.astype(jnp.float32) * attended.astype(jnp.float32), axis=1, keepdims=True
    )
    d_probs = lax.dot_general(
        do, v, (((1,), (1,)), ((), ())), preferred_element_type=jnp.float32
    )
    d_scores = (probs * (d_probs - row_delta)).astype(jnp.bfloat16)
    dq = jnp.dot(d_scores, k, preferred_element_type=jnp.float32) * factor
    dq_ref[0] = dq.astype(jnp.bfloat16)
    dk = lax.dot_general(
        d_scores, q, (((0,), (0,)), ((), ())), preferred_element_type=jnp.float32
    ) * factor
    dv = lax.dot_general(
        probs_low, do, (((0,), (0,)), ((), ())), preferred_element_type=jnp.float32
    )

    @pl.when(layer_id == 0)
    def _():
        dk_acc[...] = dk
        dv_acc[...] = dv

    @pl.when(layer_id > 0)
    def _():
        dk_acc[...] += dk
        dv_acc[...] += dv

    @pl.when(layer_id == layer_count - 1)
    def _():
        dkv_ref[:, 0] = dk_acc[...].astype(jnp.bfloat16).reshape(dkv_ref.shape[0], BLK, HD)
        dkv_ref[:, 1] = dv_acc[...].astype(jnp.bfloat16).reshape(dkv_ref.shape[0], BLK, HD)


def attend(kpos_rel, queries, douts, kv_rows, factor, head_offset):
    layer_count, tok_rows, _ = queries.shape
    slot_count, _, _, chunk_width = kv_rows.shape
    key_total = slot_count * BLK
    head_count = chunk_width // HD
    kernel = functools.partial(attend_kernel, factor=factor, layer_count=layer_count)
    tok_in = pl.BlockSpec((1, tok_rows, HD), lambda h, l: (l, 0, h + head_offset))
    tok_out = pl.BlockSpec((1, tok_rows, HD), lambda h, l: (l, 0, h))
    kv_spec = pl.BlockSpec((slot_count, 2, BLK, HD), lambda h, l: (0, 0, 0, h))
    tok_shape = (layer_count, tok_rows, chunk_width)
    return pl.pallas_call(
        kernel,
        grid=(head_count, layer_count),
        in_specs=[
            pl.BlockSpec((1, key_total), lambda h, l: (0, 0)),
            tok_in,
            tok_in,
            kv_spec,
        ],
        out_specs=[tok_out, tok_out, kv_spec],
        out_shape=[
            jax.ShapeDtypeStruct(tok_shape, jnp.bfloat16),
            jax.ShapeDtypeStruct(tok_shape, jnp.bfloat16),
            jax.ShapeDtypeStruct(kv_rows.shape, jnp.bfloat16),
        ],
        scratch_shapes=[
            pltpu.VMEM((key_total, HD), jnp.float32),
            pltpu.VMEM((key_total, HD), jnp.float32),
        ],
        compiler_params=pltpu.CompilerParams(
            dimension_semantics=("arbitrary", "arbitrary"),
            vmem_limit_bytes=48 * 1024 * 1024,
        ),
    )(kpos_rel, queries, douts, kv_rows)


def on_device(queries, cache_keys, cache_values, douts, reads):
    layer_count, tok_rows, head_width = queries.shape
    kv_rows, full_width = cache_keys.shape
    ctx_count = lax.axis_size("ctx")
    mp_count = lax.axis_size("mp")
    owner_count = ctx_count * mp_count
    per_owner = kv_rows // BLK
    my_owner = lax.axis_index(("ctx", "mp"))
    my_stretch = lax.axis_index("ctx")
    my_mp = lax.axis_index("mp")
    factor = 1.0 / math.sqrt(HD)
    spread = jnp.broadcast_to(reads, (owner_count, reads.shape[1]))
    all_lists = exchange(spread).reshape(ctx_count, mp_count, -1)[:, 0, :]
    owner_hit = (all_lists >= 0) & (all_lists // per_owner == my_owner)
    chosen = jnp.sum(jnp.where(owner_hit, all_lists - my_owner * per_owner, 0), axis=1)
    wanted = jnp.any(owner_hit, axis=1)
    picker = (chosen[:, None] == jnp.arange(per_owner, dtype=jnp.int32)[None, :]) & wanted[:, None]
    picker_low = picker.astype(jnp.bfloat16)

    def by_block(cache_rows):
        return cache_rows.reshape(per_owner, BLK, mp_count, head_width).transpose(0, 2, 1, 3)

    block_grid = jnp.stack([by_block(cache_keys), by_block(cache_values)], axis=2)
    chunk_width = (head_width // HD // 2) * HD
    chunk_grids = (block_grid[..., :chunk_width], block_grid[..., chunk_width:])

    def outgoing(chunk_grid):
        picked = jnp.zeros((ctx_count,) + chunk_grid.shape[1:], jnp.bfloat16)
        for block_id in range(per_owner):
            hit = picker[:, block_id].reshape(ctx_count, 1, 1, 1, 1)
            picked = jnp.where(hit, chunk_grid[block_id][None], picked)
        return picked.reshape((owner_count,) + chunk_grid.shape[2:])

    def absorb(returned):
        block_grid = returned.reshape((ctx_count, mp_count) + returned.shape[1:])
        return lax.dot_general(
            picker_low, block_grid, (((0,), (0,)), ((), ())), preferred_element_type=jnp.float32
        )

    own_list = reads[0]
    owner_ids = jnp.arange(owner_count, dtype=jnp.int32)
    slot_hit = (own_list[:, None] >= 0) & (own_list[:, None] // per_owner == owner_ids[None, :])
    slot_live = jnp.any(slot_hit, axis=0)
    slot_block = jnp.sum(
        jnp.where(slot_hit, own_list[:, None] - owner_ids[None, :] * per_owner, 0), axis=0
    )
    slot_start = owner_ids * kv_rows + slot_block * BLK
    key_pos = (slot_start[:, None] + jnp.arange(BLK, dtype=jnp.int32)[None, :]).reshape(-1)
    key_live = jnp.repeat(slot_live, BLK)
    kpos_rel = jnp.where(key_live, key_pos - my_stretch * tok_rows, far_pos)
    kpos_rel = kpos_rel.reshape(1, -1).astype(jnp.int32)
    src_ctx = jnp.arange(owner_count, dtype=jnp.int32) // mp_count
    kv_first = exchange(outgoing(chunk_grids[0]))
    out_first, dq_first, grads_first = attend(kpos_rel, queries, douts, kv_first, factor, 0)
    later = (src_ctx >= my_stretch).reshape(owner_count, 1, 1, 1)
    mixed = exchange(jnp.where(later, outgoing(chunk_grids[1]), grads_first))
    own_grads = lax.dynamic_slice_in_dim(grads_first, my_stretch * mp_count, mp_count, 0)
    own_back = lax.all_to_all(own_grads, "mp", split_axis=0, concat_axis=0, tiled=True)
    back_first = lax.dynamic_update_slice_in_dim(mixed, own_back, my_stretch * mp_count, 0)
    head_offset = chunk_width // HD
    out_second, dq_second, grads_second = attend(
        kpos_rel, queries, douts, mixed, factor, head_offset
    )
    back_second = exchange(grads_second)
    summed = jnp.concatenate([absorb(back_first), absorb(back_second)], axis=-1)
    summed = summed.transpose(2, 0, 3, 1, 4).reshape(2, kv_rows, full_width)
    attended = jnp.concatenate([out_first, out_second], axis=-1)
    d_query = jnp.concatenate([dq_first, dq_second], axis=-1)
    return (attended, d_query, summed[0], summed[1])


def solution(mesh):
    return jax.shard_map(
        on_device,
        mesh=mesh,
        in_specs=(
            P(None, "ctx", "mp"),
            P(("ctx", "mp"), None),
            P(("ctx", "mp"), None),
            P(None, "ctx", "mp"),
            P("ctx", None),
        ),
        out_specs=(
            P(None, "ctx", "mp"),
            P(None, "ctx", "mp"),
            P(("ctx", "mp"), None),
            P(("ctx", "mp"), None),
        ),
        check_vma=False,
    )
```

```python
import functools
import math

import jax
import jax.numpy as jnp
from jax import lax
from jax.experimental import pallas as pl
from jax.experimental.pallas import tpu as pltpu
from jax.sharding import PartitionSpec as P

HD = 128
BLK = 16

neg_big = -1e30
far_pos = 1 << 30
chunk_count = 5


def exchange(operand):
    return lax.all_to_all(operand, ("ctx", "mp"), split_axis=0, concat_axis=0, tiled=True)


def attend_kernel(
    kpos_ref, q_ref, do_ref, kv_ref, o_ref, dq_ref, dkv_ref, dk_acc, dv_acc,
    *, factor, layer_count
):
    layer_id = pl.program_id(1)
    q = q_ref[0]
    do = do_ref[0]
    key_total = dk_acc.shape[0]
    k = kv_ref[:, 0].reshape(key_total, HD)
    v = kv_ref[:, 1].reshape(key_total, HD)
    tok_rows = q.shape[0]
    rows = lax.broadcasted_iota(jnp.int32, (tok_rows, 1), 0)
    visible = kpos_ref[...] <= rows
    scores = lax.dot_general(
        q, k, (((1,), (1,)), ((), ())), preferred_element_type=jnp.float32
    ) * factor
    scores = jnp.where(visible, scores, neg_big)
    row_top = jnp.max(scores, axis=1, keepdims=True)
    raised = jnp.exp(scores - row_top)
    row_total = jnp.sum(raised, axis=1, keepdims=True)
    probs = raised * (1.0 / row_total)
    probs_low = probs.astype(jnp.bfloat16)
    attended = jnp.dot(probs_low, v, preferred_element_type=jnp.float32).astype(jnp.bfloat16)
    o_ref[0] = attended
    row_delta = jnp.sum(
        do.astype(jnp.float32) * attended.astype(jnp.float32), axis=1, keepdims=True
    )
    d_probs = lax.dot_general(
        do, v, (((1,), (1,)), ((), ())), preferred_element_type=jnp.float32
    )
    d_scores = (probs * (d_probs - row_delta)).astype(jnp.bfloat16)
    dq = jnp.dot(d_scores, k, preferred_element_type=jnp.float32) * factor
    dq_ref[0] = dq.astype(jnp.bfloat16)
    dk = lax.dot_general(
        d_scores, q, (((0,), (0,)), ((), ())), preferred_element_type=jnp.float32
    ) * factor
    dv = lax.dot_general(
        probs_low, do, (((0,), (0,)), ((), ())), preferred_element_type=jnp.float32
    )

    @pl.when(layer_id == 0)
    def _():
        dk_acc[...] = dk
        dv_acc[...] = dv

    @pl.when(layer_id > 0)
    def _():
        dk_acc[...] += dk
        dv_acc[...] += dv

    @pl.when(layer_id == layer_count - 1)
    def _():
        dkv_ref[:, 0] = dk_acc[...].astype(jnp.bfloat16).reshape(dkv_ref.shape[0], BLK, HD)
        dkv_ref[:, 1] = dv_acc[...].astype(jnp.bfloat16).reshape(dkv_ref.shape[0], BLK, HD)


def attend(kpos_rel, queries, douts, kv_rows, factor, head_offset):
    layer_count, tok_rows, _ = queries.shape
    slot_count, _, _, chunk_width = kv_rows.shape
    key_total = slot_count * BLK
    head_count = chunk_width // HD
    kernel = functools.partial(attend_kernel, factor=factor, layer_count=layer_count)
    tok_in = pl.BlockSpec((1, tok_rows, HD), lambda h, l: (l, 0, h + head_offset))
    tok_out = pl.BlockSpec((1, tok_rows, HD), lambda h, l: (l, 0, h))
    kv_spec = pl.BlockSpec((slot_count, 2, BLK, HD), lambda h, l: (0, 0, 0, h))
    tok_shape = (layer_count, tok_rows, chunk_width)
    return pl.pallas_call(
        kernel,
        grid=(head_count, layer_count),
        in_specs=[
            pl.BlockSpec((1, key_total), lambda h, l: (0, 0)),
            tok_in,
            tok_in,
            kv_spec,
        ],
        out_specs=[tok_out, tok_out, kv_spec],
        out_shape=[
            jax.ShapeDtypeStruct(tok_shape, jnp.bfloat16),
            jax.ShapeDtypeStruct(tok_shape, jnp.bfloat16),
            jax.ShapeDtypeStruct(kv_rows.shape, jnp.bfloat16),
        ],
        scratch_shapes=[
            pltpu.VMEM((key_total, HD), jnp.float32),
            pltpu.VMEM((key_total, HD), jnp.float32),
        ],
        compiler_params=pltpu.CompilerParams(
            dimension_semantics=("arbitrary", "arbitrary"),
            vmem_limit_bytes=48 * 1024 * 1024,
        ),
    )(kpos_rel, queries, douts, kv_rows)


def on_device(queries, cache_keys, cache_values, douts, reads):
    layer_count, tok_rows, head_width = queries.shape
    kv_rows, full_width = cache_keys.shape
    ctx_count = lax.axis_size("ctx")
    mp_count = lax.axis_size("mp")
    owner_count = ctx_count * mp_count
    per_owner = kv_rows // BLK
    my_owner = lax.axis_index(("ctx", "mp"))
    my_stretch = lax.axis_index("ctx")
    my_mp = lax.axis_index("mp")
    factor = 1.0 / math.sqrt(HD)
    spread = jnp.broadcast_to(reads, (owner_count, reads.shape[1]))
    all_lists = exchange(spread).reshape(ctx_count, mp_count, -1)[:, 0, :]
    owner_hit = (all_lists >= 0) & (all_lists // per_owner == my_owner)
    chosen = jnp.sum(jnp.where(owner_hit, all_lists - my_owner * per_owner, 0), axis=1)
    wanted = jnp.any(owner_hit, axis=1)
    picker = (chosen[:, None] == jnp.arange(per_owner, dtype=jnp.int32)[None, :]) & wanted[:, None]
    picker_low = picker.astype(jnp.bfloat16)

    def by_block(cache_rows):
        return cache_rows.reshape(per_owner, BLK, mp_count, head_width).transpose(0, 2, 1, 3)

    block_grid = jnp.stack([by_block(cache_keys), by_block(cache_values)], axis=2)
    chunk_width = head_width // chunk_count
    chunk_grids = [
        block_grid[..., part * chunk_width:(part + 1) * chunk_width] for part in range(chunk_count)
    ]

    def outgoing(chunk_grid):
        picked = jnp.zeros((ctx_count,) + chunk_grid.shape[1:], jnp.bfloat16)
        for block_id in range(per_owner):
            hit = picker[:, block_id].reshape(ctx_count, 1, 1, 1, 1)
            picked = jnp.where(hit, chunk_grid[block_id][None], picked)
        return picked.reshape((owner_count,) + chunk_grid.shape[2:])

    def absorb(returned):
        block_grid = returned.reshape((ctx_count, mp_count) + returned.shape[1:])
        return lax.dot_general(
            picker_low, block_grid, (((0,), (0,)), ((), ())), preferred_element_type=jnp.float32
        )

    own_list = reads[0]
    owner_ids = jnp.arange(owner_count, dtype=jnp.int32)
    slot_hit = (own_list[:, None] >= 0) & (own_list[:, None] // per_owner == owner_ids[None, :])
    slot_live = jnp.any(slot_hit, axis=0)
    slot_block = jnp.sum(
        jnp.where(slot_hit, own_list[:, None] - owner_ids[None, :] * per_owner, 0), axis=0
    )
    slot_start = owner_ids * kv_rows + slot_block * BLK
    key_pos = (slot_start[:, None] + jnp.arange(BLK, dtype=jnp.int32)[None, :]).reshape(-1)
    key_live = jnp.repeat(slot_live, BLK)
    kpos_rel = jnp.where(key_live, key_pos - my_stretch * tok_rows, far_pos)
    kpos_rel = kpos_rel.reshape(1, -1).astype(jnp.int32)
    dest_ctx = jnp.arange(owner_count, dtype=jnp.int32) // mp_count
    later = (dest_ctx >= my_stretch).reshape(owner_count, 1, 1, 1)
    heads_per_chunk = chunk_width // HD
    received = exchange(outgoing(chunk_grids[0]))
    outs, dqs, absorbed = [], [], []
    for part in range(chunk_count):
        out_part, dq_part, grads_part = attend(
            kpos_rel, queries, douts, received, factor, part * heads_per_chunk
        )
        outs.append(out_part)
        dqs.append(dq_part)
        if part + 1 < chunk_count:
            received = exchange(jnp.where(later, outgoing(chunk_grids[part + 1]), grads_part))
            own_grads = lax.dynamic_slice_in_dim(grads_part, my_stretch * mp_count, mp_count, 0)
            own_back = lax.all_to_all(own_grads, "mp", split_axis=0, concat_axis=0, tiled=True)
            back = lax.dynamic_update_slice_in_dim(received, own_back, my_stretch * mp_count, 0)
        else:
            back = exchange(grads_part)
        absorbed.append(absorb(back))
    summed = jnp.concatenate(absorbed, axis=-1)
    summed = summed.transpose(2, 0, 3, 1, 4).reshape(2, kv_rows, full_width)
    attended = jnp.concatenate(outs, axis=-1)
    d_query = jnp.concatenate(dqs, axis=-1)
    return (attended, d_query, summed[0], summed[1])


def solution(mesh):
    return jax.shard_map(
        on_device,
        mesh=mesh,
        in_specs=(
            P(None, "ctx", "mp"),
            P(("ctx", "mp"), None),
            P(("ctx", "mp"), None),
            P(None, "ctx", "mp"),
            P("ctx", None),
        ),
        out_specs=(
            P(None, "ctx", "mp"),
            P(None, "ctx", "mp"),
            P(("ctx", "mp"), None),
            P(("ctx", "mp"), None),
        ),
        check_vma=False,
    )
```

```python
import functools
import math

import jax
import jax.numpy as jnp
from jax import lax
from jax.experimental import pallas as pl
from jax.experimental.pallas import tpu as pltpu
from jax.sharding import PartitionSpec as P

HD = 128
BLK = 16

neg_big = -1e30
far_pos = 1 << 30


def exchange(operand):
    return lax.all_to_all(operand, ("ctx", "mp"), split_axis=0, concat_axis=0, tiled=True)


def attend_kernel(*refs, factor, layer_count, mixed):
    if mixed:
        split_ref, kpos_ref, q_ref, do_ref, kv_ref, next_ref = refs[:6]
        o_ref, dq_ref, dkv_ref, own_ref, dk_acc, dv_acc = refs[6:]
    else:
        kpos_ref, q_ref, do_ref, kv_ref = refs[:4]
        o_ref, dq_ref, dkv_ref, dk_acc, dv_acc = refs[4:]
    layer_id = pl.program_id(1)
    q = q_ref[0]
    do = do_ref[0]
    key_total = dk_acc.shape[0]
    k = kv_ref[:, 0].reshape(key_total, HD)
    v = kv_ref[:, 1].reshape(key_total, HD)
    tok_rows = q.shape[0]
    rows = lax.broadcasted_iota(jnp.int32, (tok_rows, 1), 0)
    visible = kpos_ref[...] <= rows
    scores = lax.dot_general(
        q, k, (((1,), (1,)), ((), ())), preferred_element_type=jnp.float32
    ) * factor
    scores = jnp.where(visible, scores, neg_big)
    row_top = jnp.max(scores, axis=1, keepdims=True)
    raised = jnp.exp(scores - row_top)
    row_total = jnp.sum(raised, axis=1, keepdims=True)
    probs = raised * (1.0 / row_total)
    probs_low = probs.astype(jnp.bfloat16)
    attended = jnp.dot(probs_low, v, preferred_element_type=jnp.float32).astype(jnp.bfloat16)
    o_ref[0] = attended
    row_delta = jnp.sum(
        do.astype(jnp.float32) * attended.astype(jnp.float32), axis=1, keepdims=True
    )
    d_probs = lax.dot_general(
        do, v, (((1,), (1,)), ((), ())), preferred_element_type=jnp.float32
    )
    d_scores = (probs * (d_probs - row_delta)).astype(jnp.bfloat16)
    dq = jnp.dot(d_scores, k, preferred_element_type=jnp.float32) * factor
    dq_ref[0] = dq.astype(jnp.bfloat16)
    dk = lax.dot_general(
        d_scores, q, (((0,), (0,)), ((), ())), preferred_element_type=jnp.float32
    ) * factor
    dv = lax.dot_general(
        probs_low, do, (((0,), (0,)), ((), ())), preferred_element_type=jnp.float32
    )

    @pl.when(layer_id == 0)
    def _():
        dk_acc[...] = dk
        dv_acc[...] = dv

    @pl.when(layer_id > 0)
    def _():
        dk_acc[...] += dk
        dv_acc[...] += dv

    @pl.when(layer_id == layer_count - 1)
    def _():
        slot_count = dkv_ref.shape[0]
        dk_low = dk_acc[...].astype(jnp.bfloat16).reshape(slot_count, BLK, HD)
        dv_low = dv_acc[...].astype(jnp.bfloat16).reshape(slot_count, BLK, HD)
        if mixed:
            own_count = own_ref.shape[0]
            start_row = pl.multiple_of(split_ref[0] * BLK, own_count * BLK)
            own_k = dk_acc[pl.ds(start_row, own_count * BLK), :].astype(jnp.bfloat16)
            own_v = dv_acc[pl.ds(start_row, own_count * BLK), :].astype(jnp.bfloat16)
            own_ref[:, 0] = own_k.reshape(own_count, BLK, HD)
            own_ref[:, 1] = own_v.reshape(own_count, BLK, HD)
            slot_ids = lax.broadcasted_iota(jnp.int32, (slot_count, BLK, HD), 0)
            later = slot_ids >= split_ref[0]
            dk_low = jnp.where(later, next_ref[:, 0], dk_low)
            dv_low = jnp.where(later, next_ref[:, 1], dv_low)
        dkv_ref[:, 0] = dk_low
        dkv_ref[:, 1] = dv_low


def attend(
    kpos_rel, queries, douts, kv_rows, factor, head_offset, split=None, next_rows=None,
    own_slots=None,
):
    layer_count, tok_rows, _ = queries.shape
    slot_count, _, _, chunk_width = kv_rows.shape
    key_total = slot_count * BLK
    head_count = chunk_width // HD
    mixed = next_rows is not None
    kernel = functools.partial(
        attend_kernel, factor=factor, layer_count=layer_count, mixed=mixed
    )
    tok_in = pl.BlockSpec((1, tok_rows, HD), lambda h, l: (l, 0, h + head_offset))
    tok_out = pl.BlockSpec((1, tok_rows, HD), lambda h, l: (l, 0, h))
    kv_spec = pl.BlockSpec((slot_count, 2, BLK, HD), lambda h, l: (0, 0, 0, h))
    tok_shape = (layer_count, tok_rows, chunk_width)
    in_specs = [pl.BlockSpec((1, key_total), lambda h, l: (0, 0)), tok_in, tok_in, kv_spec]
    operands = [kpos_rel, queries, douts, kv_rows]
    out_specs = [tok_out, tok_out, kv_spec]
    out_shape = [
        jax.ShapeDtypeStruct(tok_shape, jnp.bfloat16),
        jax.ShapeDtypeStruct(tok_shape, jnp.bfloat16),
        jax.ShapeDtypeStruct(kv_rows.shape, jnp.bfloat16),
    ]
    if mixed:
        in_specs = [pl.BlockSpec(memory_space=pltpu.SMEM)] + in_specs + [kv_spec]
        operands = [split] + operands + [next_rows]
        own_count = own_slots
        out_specs.append(pl.BlockSpec((own_count, 2, BLK, HD), lambda h, l: (0, 0, 0, h)))
        out_shape.append(jax.ShapeDtypeStruct((own_count, 2, BLK, chunk_width), jnp.bfloat16))
    return pl.pallas_call(
        kernel,
        grid=(head_count, layer_count),
        in_specs=in_specs,
        out_specs=out_specs,
        out_shape=out_shape,
        scratch_shapes=[
            pltpu.VMEM((key_total, HD), jnp.float32),
            pltpu.VMEM((key_total, HD), jnp.float32),
        ],
        compiler_params=pltpu.CompilerParams(
            dimension_semantics=("arbitrary", "arbitrary"),
            vmem_limit_bytes=48 * 1024 * 1024,
        ),
    )(*operands)


def on_device(queries, cache_keys, cache_values, douts, reads):
    layer_count, tok_rows, head_width = queries.shape
    kv_rows, full_width = cache_keys.shape
    ctx_count = lax.axis_size("ctx")
    mp_count = lax.axis_size("mp")
    owner_count = ctx_count * mp_count
    per_owner = kv_rows // BLK
    my_owner = lax.axis_index(("ctx", "mp"))
    my_stretch = lax.axis_index("ctx")
    my_mp = lax.axis_index("mp")
    factor = 1.0 / math.sqrt(HD)
    spread = jnp.broadcast_to(reads, (owner_count, reads.shape[1]))
    all_lists = exchange(spread).reshape(ctx_count, mp_count, -1)[:, 0, :]
    owner_hit = (all_lists >= 0) & (all_lists // per_owner == my_owner)
    chosen = jnp.sum(jnp.where(owner_hit, all_lists - my_owner * per_owner, 0), axis=1)
    wanted = jnp.any(owner_hit, axis=1)
    picker = (chosen[:, None] == jnp.arange(per_owner, dtype=jnp.int32)[None, :]) & wanted[:, None]
    picker_low = picker.astype(jnp.bfloat16)

    def by_block(cache_rows):
        return cache_rows.reshape(per_owner, BLK, mp_count, head_width).transpose(0, 2, 1, 3)

    block_grid = jnp.stack([by_block(cache_keys), by_block(cache_values)], axis=2)
    chunk_width = (head_width // HD // 2) * HD
    chunk_grids = (block_grid[..., :chunk_width], block_grid[..., chunk_width:])

    def outgoing(chunk_grid):
        picked = jnp.zeros((ctx_count,) + chunk_grid.shape[1:], jnp.bfloat16)
        for block_id in range(per_owner):
            hit = picker[:, block_id].reshape(ctx_count, 1, 1, 1, 1)
            picked = jnp.where(hit, chunk_grid[block_id][None], picked)
        return picked.reshape((owner_count,) + chunk_grid.shape[2:])

    def absorb(returned):
        block_grid = returned.reshape((ctx_count, mp_count) + returned.shape[1:])
        return lax.dot_general(
            picker_low, block_grid, (((0,), (0,)), ((), ())), preferred_element_type=jnp.float32
        )

    own_list = reads[0]
    owner_ids = jnp.arange(owner_count, dtype=jnp.int32)
    slot_hit = (own_list[:, None] >= 0) & (own_list[:, None] // per_owner == owner_ids[None, :])
    slot_live = jnp.any(slot_hit, axis=0)
    slot_block = jnp.sum(
        jnp.where(slot_hit, own_list[:, None] - owner_ids[None, :] * per_owner, 0), axis=0
    )
    slot_start = owner_ids * kv_rows + slot_block * BLK
    key_pos = (slot_start[:, None] + jnp.arange(BLK, dtype=jnp.int32)[None, :]).reshape(-1)
    key_live = jnp.repeat(slot_live, BLK)
    kpos_rel = jnp.where(key_live, key_pos - my_stretch * tok_rows, far_pos)
    kpos_rel = kpos_rel.reshape(1, -1).astype(jnp.int32)
    split = (my_stretch * mp_count).reshape(1).astype(jnp.int32)
    kv_first = exchange(outgoing(chunk_grids[0]))
    out_first, dq_first, mixed_first, own_grads = attend(
        kpos_rel, queries, douts, kv_first, factor, 0, split, outgoing(chunk_grids[1]),
        mp_count,
    )
    kv_second = exchange(mixed_first)
    own_back = lax.all_to_all(own_grads, "mp", split_axis=0, concat_axis=0, tiled=True)
    back_first = lax.dynamic_update_slice_in_dim(kv_second, own_back, my_stretch * mp_count, 0)
    head_offset = chunk_width // HD
    out_second, dq_second, grads_second = attend(
        kpos_rel, queries, douts, kv_second, factor, head_offset
    )
    back_second = exchange(grads_second)
    summed = jnp.concatenate([absorb(back_first), absorb(back_second)], axis=-1)
    summed = summed.transpose(2, 0, 3, 1, 4).reshape(2, kv_rows, full_width)
    attended = jnp.concatenate([out_first, out_second], axis=-1)
    d_query = jnp.concatenate([dq_first, dq_second], axis=-1)
    return (attended, d_query, summed[0], summed[1])


def solution(mesh):
    return jax.shard_map(
        on_device,
        mesh=mesh,
        in_specs=(
            P(None, "ctx", "mp"),
            P(("ctx", "mp"), None),
            P(("ctx", "mp"), None),
            P(None, "ctx", "mp"),
            P("ctx", None),
        ),
        out_specs=(
            P(None, "ctx", "mp"),
            P(None, "ctx", "mp"),
            P(("ctx", "mp"), None),
            P(("ctx", "mp"), None),
        ),
        check_vma=False,
    )
```

```python
import functools
import math

import jax
import jax.numpy as jnp
from jax import lax
from jax.experimental import pallas as pl
from jax.experimental.pallas import tpu as pltpu
from jax.sharding import PartitionSpec as P

HD = 128
BLK = 16

neg_big = -1e30
far_pos = 1 << 30


def exchange(operand):
    return lax.all_to_all(operand, ("ctx", "mp"), split_axis=0, concat_axis=0, tiled=True)


def attend_kernel(*refs, factor, layer_count, mixed):
    if mixed:
        split_ref, kpos_ref, q_ref, do_ref, kv_ref, next_ref = refs[:6]
        o_ref, dq_ref, dkv_ref, own_ref, dk_acc, dv_acc = refs[6:]
    else:
        kpos_ref, q_ref, do_ref, kv_ref = refs[:4]
        o_ref, dq_ref, dkv_ref, dk_acc, dv_acc = refs[4:]
    layer_id = pl.program_id(1)
    q = q_ref[0]
    do = do_ref[0]
    key_total = dk_acc.shape[0]
    k = kv_ref[:, 0].reshape(key_total, HD)
    v = kv_ref[:, 1].reshape(key_total, HD)
    tok_rows = q.shape[0]
    rows = lax.broadcasted_iota(jnp.int32, (tok_rows, 1), 0)
    visible = kpos_ref[...] <= rows
    scores = lax.dot_general(
        q, k, (((1,), (1,)), ((), ())), preferred_element_type=jnp.float32
    ) * factor
    scores = jnp.where(visible, scores, neg_big)
    row_top = jnp.max(scores, axis=1, keepdims=True)
    raised = jnp.exp(scores - row_top)
    row_total = jnp.sum(raised, axis=1, keepdims=True)
    probs = raised * (1.0 / row_total)
    probs_low = probs.astype(jnp.bfloat16)
    attended = jnp.dot(probs_low, v, preferred_element_type=jnp.float32).astype(jnp.bfloat16)
    o_ref[0] = attended
    row_delta = jnp.sum(
        do.astype(jnp.float32) * attended.astype(jnp.float32), axis=1, keepdims=True
    )
    d_probs = lax.dot_general(
        do, v, (((1,), (1,)), ((), ())), preferred_element_type=jnp.float32
    )
    d_scores = (probs * (d_probs - row_delta)).astype(jnp.bfloat16)
    dq = jnp.dot(d_scores, k, preferred_element_type=jnp.float32) * factor
    dq_ref[0] = dq.astype(jnp.bfloat16)
    dk = lax.dot_general(
        d_scores, q, (((0,), (0,)), ((), ())), preferred_element_type=jnp.float32
    ) * factor
    dv = lax.dot_general(
        probs_low, do, (((0,), (0,)), ((), ())), preferred_element_type=jnp.float32
    )

    @pl.when(layer_id == 0)
    def _():
        dk_acc[...] = dk
        dv_acc[...] = dv

    @pl.when(layer_id > 0)
    def _():
        dk_acc[...] += dk
        dv_acc[...] += dv

    @pl.when(layer_id == layer_count - 1)
    def _():
        slot_count = dkv_ref.shape[0]
        dk_low = dk_acc[...].astype(jnp.bfloat16).reshape(slot_count, BLK, HD)
        dv_low = dv_acc[...].astype(jnp.bfloat16).reshape(slot_count, BLK, HD)
        if mixed:
            own_count = own_ref.shape[0]
            start_row = pl.multiple_of(split_ref[0] * BLK, own_count * BLK)
            own_k = dk_acc[pl.ds(start_row, own_count * BLK), :].astype(jnp.bfloat16)
            own_v = dv_acc[pl.ds(start_row, own_count * BLK), :].astype(jnp.bfloat16)
            own_ref[:, 0] = own_k.reshape(own_count, BLK, HD)
            own_ref[:, 1] = own_v.reshape(own_count, BLK, HD)
            slot_ids = lax.broadcasted_iota(jnp.int32, (slot_count, BLK, HD), 0)
            later = slot_ids >= split_ref[0]
            dk_low = jnp.where(later, next_ref[:, 0], dk_low)
            dv_low = jnp.where(later, next_ref[:, 1], dv_low)
        dkv_ref[:, 0] = dk_low
        dkv_ref[:, 1] = dv_low


def attend(
    kpos_rel, queries, douts, kv_rows, factor, head_offset, split=None, next_rows=None,
    own_slots=None,
):
    layer_count, tok_rows, _ = queries.shape
    slot_count, _, _, chunk_width = kv_rows.shape
    key_total = slot_count * BLK
    head_count = chunk_width // HD
    mixed = next_rows is not None
    kernel = functools.partial(
        attend_kernel, factor=factor, layer_count=layer_count, mixed=mixed
    )
    tok_in = pl.BlockSpec((1, tok_rows, HD), lambda h, l: (l, 0, h + head_offset))
    tok_out = pl.BlockSpec((1, tok_rows, HD), lambda h, l: (l, 0, h))
    kv_spec = pl.BlockSpec((slot_count, 2, BLK, HD), lambda h, l: (0, 0, 0, h))
    tok_shape = (layer_count, tok_rows, chunk_width)
    in_specs = [pl.BlockSpec((1, key_total), lambda h, l: (0, 0)), tok_in, tok_in, kv_spec]
    operands = [kpos_rel, queries, douts, kv_rows]
    out_specs = [tok_out, tok_out, kv_spec]
    out_shape = [
        jax.ShapeDtypeStruct(tok_shape, jnp.bfloat16),
        jax.ShapeDtypeStruct(tok_shape, jnp.bfloat16),
        jax.ShapeDtypeStruct(kv_rows.shape, jnp.bfloat16),
    ]
    if mixed:
        in_specs = [pl.BlockSpec(memory_space=pltpu.SMEM)] + in_specs + [kv_spec]
        operands = [split] + operands + [next_rows]
        own_count = own_slots
        out_specs.append(pl.BlockSpec((own_count, 2, BLK, HD), lambda h, l: (0, 0, 0, h)))
        out_shape.append(jax.ShapeDtypeStruct((own_count, 2, BLK, chunk_width), jnp.bfloat16))
    return pl.pallas_call(
        kernel,
        grid=(head_count, layer_count),
        in_specs=in_specs,
        out_specs=out_specs,
        out_shape=out_shape,
        scratch_shapes=[
            pltpu.VMEM((key_total, HD), jnp.float32),
            pltpu.VMEM((key_total, HD), jnp.float32),
        ],
        compiler_params=pltpu.CompilerParams(
            dimension_semantics=("arbitrary", "arbitrary"),
            vmem_limit_bytes=48 * 1024 * 1024,
        ),
    )(*operands)


def on_device(queries, cache_keys, cache_values, douts, reads):
    layer_count, tok_rows, head_width = queries.shape
    kv_rows, full_width = cache_keys.shape
    ctx_count = lax.axis_size("ctx")
    mp_count = lax.axis_size("mp")
    owner_count = ctx_count * mp_count
    per_owner = kv_rows // BLK
    my_owner = lax.axis_index(("ctx", "mp"))
    my_stretch = lax.axis_index("ctx")
    my_mp = lax.axis_index("mp")
    factor = 1.0 / math.sqrt(HD)
    spread = jnp.broadcast_to(reads, (owner_count, reads.shape[1]))
    all_lists = exchange(spread).reshape(ctx_count, mp_count, -1)[:, 0, :]
    owner_hit = (all_lists >= 0) & (all_lists // per_owner == my_owner)
    chosen = jnp.sum(jnp.where(owner_hit, all_lists - my_owner * per_owner, 0), axis=1)
    wanted = jnp.any(owner_hit, axis=1)
    picker = (chosen[:, None] == jnp.arange(per_owner, dtype=jnp.int32)[None, :]) & wanted[:, None]
    picker_low = picker.astype(jnp.bfloat16)

    def by_block(cache_rows):
        return cache_rows.reshape(per_owner, BLK, mp_count, head_width).transpose(0, 2, 1, 3)

    block_grid = jnp.stack([by_block(cache_keys), by_block(cache_values)], axis=2)
    head_count = head_width // HD
    outer_width = (2 * head_count // 5) * HD
    bounds = (0, outer_width, head_width - outer_width, head_width)
    chunk_grids = [block_grid[..., bounds[i]:bounds[i + 1]] for i in range(3)]

    def outgoing(chunk_grid):
        picked = jnp.zeros((ctx_count,) + chunk_grid.shape[1:], jnp.bfloat16)
        for block_id in range(per_owner):
            hit = picker[:, block_id].reshape(ctx_count, 1, 1, 1, 1)
            picked = jnp.where(hit, chunk_grid[block_id][None], picked)
        return picked.reshape((owner_count,) + chunk_grid.shape[2:])

    def absorb(returned):
        block_grid = returned.reshape((ctx_count, mp_count) + returned.shape[1:])
        return lax.dot_general(
            picker_low, block_grid, (((0,), (0,)), ((), ())), preferred_element_type=jnp.float32
        )

    own_list = reads[0]
    owner_ids = jnp.arange(owner_count, dtype=jnp.int32)
    slot_hit = (own_list[:, None] >= 0) & (own_list[:, None] // per_owner == owner_ids[None, :])
    slot_live = jnp.any(slot_hit, axis=0)
    slot_block = jnp.sum(
        jnp.where(slot_hit, own_list[:, None] - owner_ids[None, :] * per_owner, 0), axis=0
    )
    slot_start = owner_ids * kv_rows + slot_block * BLK
    key_pos = (slot_start[:, None] + jnp.arange(BLK, dtype=jnp.int32)[None, :]).reshape(-1)
    key_live = jnp.repeat(slot_live, BLK)
    kpos_rel = jnp.where(key_live, key_pos - my_stretch * tok_rows, far_pos)
    kpos_rel = kpos_rel.reshape(1, -1).astype(jnp.int32)
    split = (my_stretch * mp_count).reshape(1).astype(jnp.int32)
    offsets = [bound // HD for bound in bounds]
    kv_first = exchange(outgoing(chunk_grids[0]))
    kv_middle = exchange(outgoing(chunk_grids[1]))
    out_first, dq_first, mixed_first, own_grads = attend(
        kpos_rel, queries, douts, kv_first, factor, offsets[0], split,
        outgoing(chunk_grids[2]), mp_count,
    )
    kv_middle, mixed_first = lax.optimization_barrier((kv_middle, mixed_first))
    kv_last = exchange(mixed_first)
    out_middle, dq_middle, grads_middle = attend(
        kpos_rel, queries, douts, kv_middle, factor, offsets[1]
    )
    back_middle = exchange(grads_middle)
    own_back = lax.all_to_all(own_grads, "mp", split_axis=0, concat_axis=0, tiled=True)
    back_first = lax.dynamic_update_slice_in_dim(kv_last, own_back, my_stretch * mp_count, 0)
    out_last, dq_last, grads_last = attend(
        kpos_rel, queries, douts, kv_last, factor, offsets[2]
    )
    back_last = exchange(grads_last)
    summed = jnp.concatenate(
        [absorb(back_first), absorb(back_middle), absorb(back_last)], axis=-1
    )
    summed = summed.transpose(2, 0, 3, 1, 4).reshape(2, kv_rows, full_width)
    attended = jnp.concatenate([out_first, out_middle, out_last], axis=-1)
    d_query = jnp.concatenate([dq_first, dq_middle, dq_last], axis=-1)
    return (attended, d_query, summed[0], summed[1])


def solution(mesh):
    return jax.shard_map(
        on_device,
        mesh=mesh,
        in_specs=(
            P(None, "ctx", "mp"),
            P(("ctx", "mp"), None),
            P(("ctx", "mp"), None),
            P(None, "ctx", "mp"),
            P("ctx", None),
        ),
        out_specs=(
            P(None, "ctx", "mp"),
            P(None, "ctx", "mp"),
            P(("ctx", "mp"), None),
            P(("ctx", "mp"), None),
        ),
        check_vma=False,
    )
```

```python
import functools
import math

import jax
import jax.numpy as jnp
from jax import lax
from jax.experimental import pallas as pl
from jax.experimental.pallas import tpu as pltpu
from jax.sharding import PartitionSpec as P

HD = 128
BLK = 16

neg_big = -1e30
far_pos = 1 << 30


def exchange(operand):
    return lax.all_to_all(operand, ("ctx", "mp"), split_axis=0, concat_axis=0, tiled=True)


def attend_kernel(*refs, factor, layer_count, mixed):
    if mixed:
        split_ref, kpos_ref, q_ref, do_ref, kv_ref, next_ref = refs[:6]
        o_ref, dq_ref, dkv_ref, own_ref, dk_acc, dv_acc = refs[6:]
    else:
        kpos_ref, q_ref, do_ref, kv_ref = refs[:4]
        o_ref, dq_ref, dkv_ref, dk_acc, dv_acc = refs[4:]
    layer_id = pl.program_id(1)
    q = q_ref[0]
    do = do_ref[0]
    key_total = dk_acc.shape[0]
    k = kv_ref[:, 0].reshape(key_total, HD)
    v = kv_ref[:, 1].reshape(key_total, HD)
    tok_rows = q.shape[0]
    rows = lax.broadcasted_iota(jnp.int32, (tok_rows, 1), 0)
    visible = kpos_ref[...] <= rows
    scores = lax.dot_general(
        q, k, (((1,), (1,)), ((), ())), preferred_element_type=jnp.float32
    ) * factor
    scores = jnp.where(visible, scores, neg_big)
    row_top = jnp.max(scores, axis=1, keepdims=True)
    raised = jnp.exp(scores - row_top)
    row_total = jnp.sum(raised, axis=1, keepdims=True)
    probs = raised * (1.0 / row_total)
    probs_low = probs.astype(jnp.bfloat16)
    attended = jnp.dot(probs_low, v, preferred_element_type=jnp.float32).astype(jnp.bfloat16)
    o_ref[0] = attended
    row_delta = jnp.sum(
        do.astype(jnp.float32) * attended.astype(jnp.float32), axis=1, keepdims=True
    )
    d_probs = lax.dot_general(
        do, v, (((1,), (1,)), ((), ())), preferred_element_type=jnp.float32
    )
    d_scores = (probs * (d_probs - row_delta)).astype(jnp.bfloat16)
    dq = jnp.dot(d_scores, k, preferred_element_type=jnp.float32) * factor
    dq_ref[0] = dq.astype(jnp.bfloat16)
    dk = lax.dot_general(
        d_scores, q, (((0,), (0,)), ((), ())), preferred_element_type=jnp.float32
    ) * factor
    dv = lax.dot_general(
        probs_low, do, (((0,), (0,)), ((), ())), preferred_element_type=jnp.float32
    )

    @pl.when(layer_id == 0)
    def _():
        dk_acc[...] = dk
        dv_acc[...] = dv

    @pl.when(layer_id > 0)
    def _():
        dk_acc[...] += dk
        dv_acc[...] += dv

    @pl.when(layer_id == layer_count - 1)
    def _():
        slot_count = dkv_ref.shape[0]
        dk_low = dk_acc[...].astype(jnp.bfloat16).reshape(slot_count, BLK, HD)
        dv_low = dv_acc[...].astype(jnp.bfloat16).reshape(slot_count, BLK, HD)
        if mixed:
            own_count = own_ref.shape[0]
            start_row = pl.multiple_of(split_ref[0] * BLK, own_count * BLK)
            own_k = dk_acc[pl.ds(start_row, own_count * BLK), :].astype(jnp.bfloat16)
            own_v = dv_acc[pl.ds(start_row, own_count * BLK), :].astype(jnp.bfloat16)
            own_ref[:, 0] = own_k.reshape(own_count, BLK, HD)
            own_ref[:, 1] = own_v.reshape(own_count, BLK, HD)
            slot_ids = lax.broadcasted_iota(jnp.int32, (slot_count, BLK, HD), 0)
            later = slot_ids >= split_ref[0]
            dk_low = jnp.where(later, next_ref[:, 0], dk_low)
            dv_low = jnp.where(later, next_ref[:, 1], dv_low)
        dkv_ref[:, 0] = dk_low
        dkv_ref[:, 1] = dv_low


def attend(
    kpos_rel, queries, douts, kv_rows, factor, head_offset, split=None, next_rows=None,
    own_slots=None,
):
    layer_count, tok_rows, _ = queries.shape
    slot_count, _, _, chunk_width = kv_rows.shape
    key_total = slot_count * BLK
    head_count = chunk_width // HD
    mixed = next_rows is not None
    kernel = functools.partial(
        attend_kernel, factor=factor, layer_count=layer_count, mixed=mixed
    )
    tok_in = pl.BlockSpec((1, tok_rows, HD), lambda h, l: (l, 0, h + head_offset))
    tok_out = pl.BlockSpec((1, tok_rows, HD), lambda h, l: (l, 0, h))
    kv_spec = pl.BlockSpec((slot_count, 2, BLK, HD), lambda h, l: (0, 0, 0, h))
    tok_shape = (layer_count, tok_rows, chunk_width)
    in_specs = [pl.BlockSpec((1, key_total), lambda h, l: (0, 0)), tok_in, tok_in, kv_spec]
    operands = [kpos_rel, queries, douts, kv_rows]
    out_specs = [tok_out, tok_out, kv_spec]
    out_shape = [
        jax.ShapeDtypeStruct(tok_shape, jnp.bfloat16),
        jax.ShapeDtypeStruct(tok_shape, jnp.bfloat16),
        jax.ShapeDtypeStruct(kv_rows.shape, jnp.bfloat16),
    ]
    if mixed:
        in_specs = [pl.BlockSpec(memory_space=pltpu.SMEM)] + in_specs + [kv_spec]
        operands = [split] + operands + [next_rows]
        own_count = own_slots
        out_specs.append(pl.BlockSpec((own_count, 2, BLK, HD), lambda h, l: (0, 0, 0, h)))
        out_shape.append(jax.ShapeDtypeStruct((own_count, 2, BLK, chunk_width), jnp.bfloat16))
    return pl.pallas_call(
        kernel,
        grid=(head_count, layer_count),
        in_specs=in_specs,
        out_specs=out_specs,
        out_shape=out_shape,
        scratch_shapes=[
            pltpu.VMEM((key_total, HD), jnp.float32),
            pltpu.VMEM((key_total, HD), jnp.float32),
        ],
        compiler_params=pltpu.CompilerParams(
            dimension_semantics=("arbitrary", "arbitrary"),
            vmem_limit_bytes=48 * 1024 * 1024,
        ),
    )(*operands)


def on_device(queries, cache_keys, cache_values, douts, reads):
    layer_count, tok_rows, head_width = queries.shape
    kv_rows, full_width = cache_keys.shape
    ctx_count = lax.axis_size("ctx")
    mp_count = lax.axis_size("mp")
    owner_count = ctx_count * mp_count
    per_owner = kv_rows // BLK
    my_owner = lax.axis_index(("ctx", "mp"))
    my_stretch = lax.axis_index("ctx")
    my_mp = lax.axis_index("mp")
    factor = 1.0 / math.sqrt(HD)
    spread = jnp.broadcast_to(reads, (owner_count, reads.shape[1]))
    all_lists = exchange(spread).reshape(ctx_count, mp_count, -1)[:, 0, :]
    owner_hit = (all_lists >= 0) & (all_lists // per_owner == my_owner)
    chosen = jnp.sum(jnp.where(owner_hit, all_lists - my_owner * per_owner, 0), axis=1)
    wanted = jnp.any(owner_hit, axis=1)
    picker = (chosen[:, None] == jnp.arange(per_owner, dtype=jnp.int32)[None, :]) & wanted[:, None]
    picker_low = picker.astype(jnp.bfloat16)

    def by_block(cache_rows):
        return cache_rows.reshape(per_owner, BLK, mp_count, head_width).transpose(0, 2, 1, 3)

    block_grid = jnp.stack([by_block(cache_keys), by_block(cache_values)], axis=2)
    head_count = head_width // HD
    outer_width = (2 * head_count // 5) * HD
    bounds = (0, outer_width, head_width - outer_width, head_width)
    chunk_grids = [block_grid[..., bounds[i]:bounds[i + 1]] for i in range(3)]

    def outgoing(chunk_grid):
        picked = jnp.zeros((ctx_count,) + chunk_grid.shape[1:], jnp.bfloat16)
        for block_id in range(per_owner):
            hit = picker[:, block_id].reshape(ctx_count, 1, 1, 1, 1)
            picked = jnp.where(hit, chunk_grid[block_id][None], picked)
        return picked.reshape((owner_count,) + chunk_grid.shape[2:])

    def absorb(returned):
        block_grid = returned.reshape((ctx_count, mp_count) + returned.shape[1:])
        return lax.dot_general(
            picker_low, block_grid, (((0,), (0,)), ((), ())), preferred_element_type=jnp.float32
        )

    own_list = reads[0]
    owner_ids = jnp.arange(owner_count, dtype=jnp.int32)
    slot_hit = (own_list[:, None] >= 0) & (own_list[:, None] // per_owner == owner_ids[None, :])
    slot_live = jnp.any(slot_hit, axis=0)
    slot_block = jnp.sum(
        jnp.where(slot_hit, own_list[:, None] - owner_ids[None, :] * per_owner, 0), axis=0
    )
    slot_start = owner_ids * kv_rows + slot_block * BLK
    key_pos = (slot_start[:, None] + jnp.arange(BLK, dtype=jnp.int32)[None, :]).reshape(-1)
    key_live = jnp.repeat(slot_live, BLK)
    kpos_rel = jnp.where(key_live, key_pos - my_stretch * tok_rows, far_pos)
    kpos_rel = kpos_rel.reshape(1, -1).astype(jnp.int32)
    split = (my_stretch * mp_count).reshape(1).astype(jnp.int32)
    offsets = [bound // HD for bound in bounds]
    kv_first = exchange(outgoing(chunk_grids[0]))
    kv_middle = exchange(outgoing(chunk_grids[1]))
    out_first, dq_first, mixed_first, own_grads = attend(
        kpos_rel, queries, douts, kv_first, factor, offsets[0], split,
        outgoing(chunk_grids[2]), mp_count,
    )
    kv_middle, mixed_first = lax.optimization_barrier((kv_middle, mixed_first))
    kv_last = exchange(mixed_first)
    out_middle, dq_middle, grads_middle = attend(
        kpos_rel, queries, douts, kv_middle, factor, offsets[1]
    )
    back_middle = exchange(grads_middle)
    gathered = lax.all_gather(own_grads, "mp", axis=0, tiled=True)
    gathered = gathered.reshape((mp_count, mp_count) + own_grads.shape[1:])
    own_back = lax.dynamic_index_in_dim(gathered, my_mp, 1, keepdims=False)
    back_first = lax.dynamic_update_slice_in_dim(kv_last, own_back, my_stretch * mp_count, 0)
    out_last, dq_last, grads_last = attend(
        kpos_rel, queries, douts, kv_last, factor, offsets[2]
    )
    back_last = exchange(grads_last)
    summed = jnp.concatenate(
        [absorb(back_first), absorb(back_middle), absorb(back_last)], axis=-1
    )
    summed = summed.transpose(2, 0, 3, 1, 4).reshape(2, kv_rows, full_width)
    attended = jnp.concatenate([out_first, out_middle, out_last], axis=-1)
    d_query = jnp.concatenate([dq_first, dq_middle, dq_last], axis=-1)
    return (attended, d_query, summed[0], summed[1])


def solution(mesh):
    return jax.shard_map(
        on_device,
        mesh=mesh,
        in_specs=(
            P(None, "ctx", "mp"),
            P(("ctx", "mp"), None),
            P(("ctx", "mp"), None),
            P(None, "ctx", "mp"),
            P("ctx", None),
        ),
        out_specs=(
            P(None, "ctx", "mp"),
            P(None, "ctx", "mp"),
            P(("ctx", "mp"), None),
            P(("ctx", "mp"), None),
        ),
        check_vma=False,
    )
```

```python
import functools
import math

import jax
import jax.numpy as jnp
from jax import lax
from jax.experimental import pallas as pl
from jax.experimental.pallas import tpu as pltpu
from jax.sharding import PartitionSpec as P

HD = 128
BLK = 16

neg_big = -1e30
far_pos = 1 << 30


def exchange(operand):
    return lax.all_to_all(operand, ("ctx", "mp"), split_axis=0, concat_axis=0, tiled=True)


def attend_kernel(*refs, factor, layer_count, mixed):
    if mixed:
        split_ref, kpos_ref, q_ref, do_ref, kv_ref, next_ref = refs[:6]
        o_ref, dq_ref, dkv_ref, own_ref, dk_acc, dv_acc = refs[6:]
    else:
        kpos_ref, q_ref, do_ref, kv_ref = refs[:4]
        o_ref, dq_ref, dkv_ref, dk_acc, dv_acc = refs[4:]
    layer_id = pl.program_id(1)
    q = q_ref[0]
    do = do_ref[0]
    key_total = dk_acc.shape[0]
    k = kv_ref[:, 0].reshape(key_total, HD)
    v = kv_ref[:, 1].reshape(key_total, HD)
    tok_rows = q.shape[0]
    rows = lax.broadcasted_iota(jnp.int32, (tok_rows, 1), 0)
    visible = kpos_ref[...] <= rows
    scores = lax.dot_general(
        q, k, (((1,), (1,)), ((), ())), preferred_element_type=jnp.float32
    ) * factor
    scores = jnp.where(visible, scores, neg_big)
    row_top = jnp.max(scores, axis=1, keepdims=True)
    raised = jnp.exp(scores - row_top)
    row_total = jnp.sum(raised, axis=1, keepdims=True)
    probs = raised * (1.0 / row_total)
    probs_low = probs.astype(jnp.bfloat16)
    attended = jnp.dot(probs_low, v, preferred_element_type=jnp.float32).astype(jnp.bfloat16)
    o_ref[0] = attended
    row_delta = jnp.sum(
        do.astype(jnp.float32) * attended.astype(jnp.float32), axis=1, keepdims=True
    )
    d_probs = lax.dot_general(
        do, v, (((1,), (1,)), ((), ())), preferred_element_type=jnp.float32
    )
    d_scores = (probs * (d_probs - row_delta)).astype(jnp.bfloat16)
    dq = jnp.dot(d_scores, k, preferred_element_type=jnp.float32) * factor
    dq_ref[0] = dq.astype(jnp.bfloat16)
    dk = lax.dot_general(
        d_scores, q, (((0,), (0,)), ((), ())), preferred_element_type=jnp.float32
    ) * factor
    dv = lax.dot_general(
        probs_low, do, (((0,), (0,)), ((), ())), preferred_element_type=jnp.float32
    )

    @pl.when(layer_id == 0)
    def _():
        dk_acc[...] = dk
        dv_acc[...] = dv

    @pl.when(layer_id > 0)
    def _():
        dk_acc[...] += dk
        dv_acc[...] += dv

    @pl.when(layer_id == layer_count - 1)
    def _():
        slot_count = dkv_ref.shape[0]
        dk_low = dk_acc[...].astype(jnp.bfloat16).reshape(slot_count, BLK, HD)
        dv_low = dv_acc[...].astype(jnp.bfloat16).reshape(slot_count, BLK, HD)
        if mixed:
            own_count = own_ref.shape[0]
            start_row = pl.multiple_of(split_ref[0] * BLK, own_count * BLK)
            own_k = dk_acc[pl.ds(start_row, own_count * BLK), :].astype(jnp.bfloat16)
            own_v = dv_acc[pl.ds(start_row, own_count * BLK), :].astype(jnp.bfloat16)
            own_ref[:, 0] = own_k.reshape(own_count, BLK, HD)
            own_ref[:, 1] = own_v.reshape(own_count, BLK, HD)
            slot_ids = lax.broadcasted_iota(jnp.int32, (slot_count, BLK, HD), 0)
            later = slot_ids >= split_ref[0]
            dk_low = jnp.where(later, next_ref[:, 0], dk_low)
            dv_low = jnp.where(later, next_ref[:, 1], dv_low)
        dkv_ref[:, 0] = dk_low
        dkv_ref[:, 1] = dv_low


def attend(
    kpos_rel, queries, douts, kv_rows, factor, head_offset, split=None, next_rows=None,
    own_slots=None,
):
    layer_count, tok_rows, _ = queries.shape
    slot_count, _, _, chunk_width = kv_rows.shape
    key_total = slot_count * BLK
    head_count = chunk_width // HD
    mixed = next_rows is not None
    kernel = functools.partial(
        attend_kernel, factor=factor, layer_count=layer_count, mixed=mixed
    )
    tok_in = pl.BlockSpec((1, tok_rows, HD), lambda h, l: (l, 0, h + head_offset))
    tok_out = pl.BlockSpec((1, tok_rows, HD), lambda h, l: (l, 0, h))
    kv_spec = pl.BlockSpec((slot_count, 2, BLK, HD), lambda h, l: (0, 0, 0, h))
    tok_shape = (layer_count, tok_rows, chunk_width)
    in_specs = [pl.BlockSpec((1, key_total), lambda h, l: (0, 0)), tok_in, tok_in, kv_spec]
    operands = [kpos_rel, queries, douts, kv_rows]
    out_specs = [tok_out, tok_out, kv_spec]
    out_shape = [
        jax.ShapeDtypeStruct(tok_shape, jnp.bfloat16),
        jax.ShapeDtypeStruct(tok_shape, jnp.bfloat16),
        jax.ShapeDtypeStruct(kv_rows.shape, jnp.bfloat16),
    ]
    if mixed:
        in_specs = [pl.BlockSpec(memory_space=pltpu.SMEM)] + in_specs + [kv_spec]
        operands = [split] + operands + [next_rows]
        own_count = own_slots
        out_specs.append(pl.BlockSpec((own_count, 2, BLK, HD), lambda h, l: (0, 0, 0, h)))
        out_shape.append(jax.ShapeDtypeStruct((own_count, 2, BLK, chunk_width), jnp.bfloat16))
    return pl.pallas_call(
        kernel,
        grid=(head_count, layer_count),
        in_specs=in_specs,
        out_specs=out_specs,
        out_shape=out_shape,
        scratch_shapes=[
            pltpu.VMEM((key_total, HD), jnp.float32),
            pltpu.VMEM((key_total, HD), jnp.float32),
        ],
        compiler_params=pltpu.CompilerParams(
            dimension_semantics=("arbitrary", "arbitrary"),
            vmem_limit_bytes=48 * 1024 * 1024,
        ),
    )(*operands)


def on_device(queries, cache_keys, cache_values, douts, reads):
    layer_count, tok_rows, head_width = queries.shape
    kv_rows, full_width = cache_keys.shape
    ctx_count = lax.axis_size("ctx")
    mp_count = lax.axis_size("mp")
    owner_count = ctx_count * mp_count
    per_owner = kv_rows // BLK
    my_owner = lax.axis_index(("ctx", "mp"))
    my_stretch = lax.axis_index("ctx")
    my_mp = lax.axis_index("mp")
    factor = 1.0 / math.sqrt(HD)
    spread = jnp.broadcast_to(reads, (owner_count, reads.shape[1]))
    all_lists = exchange(spread).reshape(ctx_count, mp_count, -1)[:, 0, :]
    owner_hit = (all_lists >= 0) & (all_lists // per_owner == my_owner)
    chosen = jnp.sum(jnp.where(owner_hit, all_lists - my_owner * per_owner, 0), axis=1)
    wanted = jnp.any(owner_hit, axis=1)
    picker = (chosen[:, None] == jnp.arange(per_owner, dtype=jnp.int32)[None, :]) & wanted[:, None]
    picker_low = picker.astype(jnp.bfloat16)

    def by_block(cache_rows):
        return cache_rows.reshape(per_owner, BLK, mp_count, head_width).transpose(0, 2, 1, 3)

    block_grid = jnp.stack([by_block(cache_keys), by_block(cache_values)], axis=2)
    head_count = head_width // HD
    outer_width = (2 * head_count // 5) * HD
    bounds = (0, outer_width, head_width - outer_width, head_width)
    chunk_grids = [block_grid[..., bounds[i]:bounds[i + 1]] for i in range(3)]

    def outgoing(chunk_grid):
        picked = jnp.zeros((ctx_count,) + chunk_grid.shape[1:], jnp.bfloat16)
        for block_id in range(per_owner):
            hit = picker[:, block_id].reshape(ctx_count, 1, 1, 1, 1)
            picked = jnp.where(hit, chunk_grid[block_id][None], picked)
        return picked.reshape((owner_count,) + chunk_grid.shape[2:])

    def absorb(returned):
        block_grid = returned.reshape((ctx_count, mp_count) + returned.shape[1:])
        return lax.dot_general(
            picker_low, block_grid, (((0,), (0,)), ((), ())), preferred_element_type=jnp.float32
        )

    own_list = reads[0]
    owner_ids = jnp.arange(owner_count, dtype=jnp.int32)
    slot_hit = (own_list[:, None] >= 0) & (own_list[:, None] // per_owner == owner_ids[None, :])
    slot_live = jnp.any(slot_hit, axis=0)
    slot_block = jnp.sum(
        jnp.where(slot_hit, own_list[:, None] - owner_ids[None, :] * per_owner, 0), axis=0
    )
    slot_start = owner_ids * kv_rows + slot_block * BLK
    key_pos = (slot_start[:, None] + jnp.arange(BLK, dtype=jnp.int32)[None, :]).reshape(-1)
    key_live = jnp.repeat(slot_live, BLK)
    kpos_rel = jnp.where(key_live, key_pos - my_stretch * tok_rows, far_pos)
    kpos_rel = kpos_rel.reshape(1, -1).astype(jnp.int32)
    split = (my_stretch * mp_count).reshape(1).astype(jnp.int32)
    offsets = [bound // HD for bound in bounds]
    kv_first = exchange(outgoing(chunk_grids[0]))
    kv_middle = exchange(outgoing(chunk_grids[1]))
    out_first, dq_first, mixed_first, own_grads = attend(
        kpos_rel, queries, douts, kv_first, factor, offsets[0], split,
        outgoing(chunk_grids[2]), mp_count,
    )
    kv_middle, mixed_first = lax.optimization_barrier((kv_middle, mixed_first))
    kv_last = exchange(mixed_first)
    out_middle, dq_middle, grads_middle = attend(
        kpos_rel, queries, douts, kv_middle, factor, offsets[1]
    )
    back_middle = exchange(grads_middle)
    own_row = jnp.arange(ctx_count, dtype=jnp.int32)[:, None] == my_stretch
    picker_others = jnp.where(own_row, jnp.zeros_like(picker_low), picker_low)
    first_rows = kv_last.reshape((ctx_count, mp_count) + kv_last.shape[1:])
    first_main = lax.dot_general(
        picker_others, first_rows, (((0,), (0,)), ((), ())), preferred_element_type=jnp.float32
    )
    middle_sum = absorb(back_middle)
    own_grads, first_main, middle_sum = lax.optimization_barrier(
        (own_grads, first_main, middle_sum)
    )
    gathered = lax.all_gather(own_grads, "mp", axis=0, tiled=True)
    gathered = gathered.reshape((mp_count, mp_count) + own_grads.shape[1:])
    own_back = lax.dynamic_index_in_dim(gathered, my_mp, 1, keepdims=False)
    own_pick = lax.dynamic_index_in_dim(picker_low, my_stretch, 0, keepdims=False)
    own_pick = own_pick.astype(jnp.float32).reshape(per_owner, 1, 1, 1, 1)
    first_sum = first_main + own_pick * own_back.astype(jnp.float32)[None]
    out_last, dq_last, grads_last = attend(
        kpos_rel, queries, douts, kv_last, factor, offsets[2]
    )
    back_last = exchange(grads_last)
    summed = jnp.concatenate([first_sum, middle_sum, absorb(back_last)], axis=-1)
    summed = summed.transpose(2, 0, 3, 1, 4).reshape(2, kv_rows, full_width)
    attended = jnp.concatenate([out_first, out_middle, out_last], axis=-1)
    d_query = jnp.concatenate([dq_first, dq_middle, dq_last], axis=-1)
    return (attended, d_query, summed[0], summed[1])


def solution(mesh):
    return jax.shard_map(
        on_device,
        mesh=mesh,
        in_specs=(
            P(None, "ctx", "mp"),
            P(("ctx", "mp"), None),
            P(("ctx", "mp"), None),
            P(None, "ctx", "mp"),
            P("ctx", None),
        ),
        out_specs=(
            P(None, "ctx", "mp"),
            P(None, "ctx", "mp"),
            P(("ctx", "mp"), None),
            P(("ctx", "mp"), None),
        ),
        check_vma=False,
    )
```

```python
import functools
import math

import jax
import jax.numpy as jnp
from jax import lax
from jax.experimental import pallas as pl
from jax.experimental.pallas import tpu as pltpu
from jax.sharding import PartitionSpec as P

HD = 128
BLK = 16

neg_big = -1e30
far_pos = 1 << 30


def exchange(operand):
    return lax.all_to_all(operand, ("ctx", "mp"), split_axis=0, concat_axis=0, tiled=True)


def attend_kernel(*refs, factor, layer_count, mixed):
    if mixed:
        split_ref, kpos_ref, q_ref, do_ref, kv_ref, next_ref = refs[:6]
        o_ref, dq_ref, dkv_ref, own_ref, dk_acc, dv_acc = refs[6:]
    else:
        kpos_ref, q_ref, do_ref, kv_ref = refs[:4]
        o_ref, dq_ref, dkv_ref, dk_acc, dv_acc = refs[4:]
    layer_id = pl.program_id(1)
    q = q_ref[0]
    do = do_ref[0]
    key_total = dk_acc.shape[0]
    k = kv_ref[:, 0].reshape(key_total, HD)
    v = kv_ref[:, 1].reshape(key_total, HD)
    tok_rows = q.shape[0]
    rows = lax.broadcasted_iota(jnp.int32, (tok_rows, 1), 0)
    visible = kpos_ref[...] <= rows
    scores = lax.dot_general(
        q, k, (((1,), (1,)), ((), ())), preferred_element_type=jnp.float32
    ) * factor
    scores = jnp.where(visible, scores, neg_big)
    row_top = jnp.max(scores, axis=1, keepdims=True)
    raised = jnp.exp(scores - row_top)
    row_total = jnp.sum(raised, axis=1, keepdims=True)
    probs = raised * (1.0 / row_total)
    probs_low = probs.astype(jnp.bfloat16)
    attended = jnp.dot(probs_low, v, preferred_element_type=jnp.float32).astype(jnp.bfloat16)
    o_ref[0] = attended
    row_delta = jnp.sum(
        do.astype(jnp.float32) * attended.astype(jnp.float32), axis=1, keepdims=True
    )
    d_probs = lax.dot_general(
        do, v, (((1,), (1,)), ((), ())), preferred_element_type=jnp.float32
    )
    d_scores = (probs * (d_probs - row_delta)).astype(jnp.bfloat16)
    dq = jnp.dot(d_scores, k, preferred_element_type=jnp.float32) * factor
    dq_ref[0] = dq.astype(jnp.bfloat16)
    dk = lax.dot_general(
        d_scores, q, (((0,), (0,)), ((), ())), preferred_element_type=jnp.float32
    ) * factor
    dv = lax.dot_general(
        probs_low, do, (((0,), (0,)), ((), ())), preferred_element_type=jnp.float32
    )

    @pl.when(layer_id == 0)
    def _():
        dk_acc[...] = dk
        dv_acc[...] = dv

    @pl.when(layer_id > 0)
    def _():
        dk_acc[...] += dk
        dv_acc[...] += dv

    @pl.when(layer_id == layer_count - 1)
    def _():
        slot_count = dkv_ref.shape[0]
        dk_low = dk_acc[...].astype(jnp.bfloat16).reshape(slot_count, BLK, HD)
        dv_low = dv_acc[...].astype(jnp.bfloat16).reshape(slot_count, BLK, HD)
        if mixed:
            own_count = own_ref.shape[0]
            start_row = pl.multiple_of(split_ref[0] * BLK, own_count * BLK)
            own_k = dk_acc[pl.ds(start_row, own_count * BLK), :].astype(jnp.bfloat16)
            own_v = dv_acc[pl.ds(start_row, own_count * BLK), :].astype(jnp.bfloat16)
            own_ref[:, 0] = own_k.reshape(own_count, BLK, HD)
            own_ref[:, 1] = own_v.reshape(own_count, BLK, HD)
            slot_ids = lax.broadcasted_iota(jnp.int32, (slot_count, BLK, HD), 0)
            later = slot_ids >= split_ref[0]
            dk_low = jnp.where(later, next_ref[:, 0], dk_low)
            dv_low = jnp.where(later, next_ref[:, 1], dv_low)
        dkv_ref[:, 0] = dk_low
        dkv_ref[:, 1] = dv_low


def attend(
    kpos_rel, queries, douts, kv_rows, factor, head_offset, split=None, next_rows=None,
    own_slots=None,
):
    layer_count, tok_rows, _ = queries.shape
    slot_count, _, _, chunk_width = kv_rows.shape
    key_total = slot_count * BLK
    head_count = chunk_width // HD
    mixed = next_rows is not None
    kernel = functools.partial(
        attend_kernel, factor=factor, layer_count=layer_count, mixed=mixed
    )
    tok_in = pl.BlockSpec((1, tok_rows, HD), lambda h, l: (l, 0, h + head_offset))
    tok_out = pl.BlockSpec((1, tok_rows, HD), lambda h, l: (l, 0, h))
    kv_spec = pl.BlockSpec((slot_count, 2, BLK, HD), lambda h, l: (0, 0, 0, h))
    tok_shape = (layer_count, tok_rows, chunk_width)
    in_specs = [pl.BlockSpec((1, key_total), lambda h, l: (0, 0)), tok_in, tok_in, kv_spec]
    operands = [kpos_rel, queries, douts, kv_rows]
    out_specs = [tok_out, tok_out, kv_spec]
    out_shape = [
        jax.ShapeDtypeStruct(tok_shape, jnp.bfloat16),
        jax.ShapeDtypeStruct(tok_shape, jnp.bfloat16),
        jax.ShapeDtypeStruct(kv_rows.shape, jnp.bfloat16),
    ]
    if mixed:
        in_specs = [pl.BlockSpec(memory_space=pltpu.SMEM)] + in_specs + [kv_spec]
        operands = [split] + operands + [next_rows]
        own_count = own_slots
        out_specs.append(pl.BlockSpec((own_count, 2, BLK, HD), lambda h, l: (0, 0, 0, h)))
        out_shape.append(jax.ShapeDtypeStruct((own_count, 2, BLK, chunk_width), jnp.bfloat16))
    return pl.pallas_call(
        kernel,
        grid=(head_count, layer_count),
        in_specs=in_specs,
        out_specs=out_specs,
        out_shape=out_shape,
        scratch_shapes=[
            pltpu.VMEM((key_total, HD), jnp.float32),
            pltpu.VMEM((key_total, HD), jnp.float32),
        ],
        compiler_params=pltpu.CompilerParams(
            dimension_semantics=("arbitrary", "arbitrary"),
            vmem_limit_bytes=48 * 1024 * 1024,
        ),
    )(*operands)


def on_device(queries, cache_keys, cache_values, douts, reads):
    layer_count, tok_rows, head_width = queries.shape
    kv_rows, full_width = cache_keys.shape
    ctx_count = lax.axis_size("ctx")
    mp_count = lax.axis_size("mp")
    owner_count = ctx_count * mp_count
    per_owner = kv_rows // BLK
    my_owner = lax.axis_index(("ctx", "mp"))
    my_stretch = lax.axis_index("ctx")
    my_mp = lax.axis_index("mp")
    factor = 1.0 / math.sqrt(HD)
    spread = jnp.broadcast_to(reads, (owner_count, reads.shape[1]))
    all_lists = exchange(spread).reshape(ctx_count, mp_count, -1)[:, 0, :]
    owner_hit = (all_lists >= 0) & (all_lists // per_owner == my_owner)
    chosen = jnp.sum(jnp.where(owner_hit, all_lists - my_owner * per_owner, 0), axis=1)
    wanted = jnp.any(owner_hit, axis=1)
    picker = (chosen[:, None] == jnp.arange(per_owner, dtype=jnp.int32)[None, :]) & wanted[:, None]
    picker_low = picker.astype(jnp.bfloat16)

    def by_block(cache_rows):
        return cache_rows.reshape(per_owner, BLK, mp_count, head_width).transpose(0, 2, 1, 3)

    block_grid = jnp.stack([by_block(cache_keys), by_block(cache_values)], axis=2)
    head_count = head_width // HD
    outer_width = (2 * head_count // 5) * HD
    bounds = (0, outer_width, head_width - outer_width, head_width)
    chunk_grids = [block_grid[..., bounds[i]:bounds[i + 1]] for i in range(3)]

    def outgoing(chunk_grid):
        picked = jnp.zeros((ctx_count,) + chunk_grid.shape[1:], jnp.bfloat16)
        for block_id in range(per_owner):
            hit = picker[:, block_id].reshape(ctx_count, 1, 1, 1, 1)
            picked = jnp.where(hit, chunk_grid[block_id][None], picked)
        return picked.reshape((owner_count,) + chunk_grid.shape[2:])

    def absorb(returned):
        block_grid = returned.reshape((ctx_count, mp_count) + returned.shape[1:])
        return lax.dot_general(
            picker_low, block_grid, (((0,), (0,)), ((), ())), preferred_element_type=jnp.float32
        )

    own_list = reads[0]
    owner_ids = jnp.arange(owner_count, dtype=jnp.int32)
    slot_hit = (own_list[:, None] >= 0) & (own_list[:, None] // per_owner == owner_ids[None, :])
    slot_live = jnp.any(slot_hit, axis=0)
    slot_block = jnp.sum(
        jnp.where(slot_hit, own_list[:, None] - owner_ids[None, :] * per_owner, 0), axis=0
    )
    slot_start = owner_ids * kv_rows + slot_block * BLK
    key_pos = (slot_start[:, None] + jnp.arange(BLK, dtype=jnp.int32)[None, :]).reshape(-1)
    key_live = jnp.repeat(slot_live, BLK)
    kpos_rel = jnp.where(key_live, key_pos - my_stretch * tok_rows, far_pos)
    kpos_rel = kpos_rel.reshape(1, -1).astype(jnp.int32)
    split = (my_stretch * mp_count).reshape(1).astype(jnp.int32)
    offsets = [bound // HD for bound in bounds]
    kv_first = exchange(outgoing(chunk_grids[0]))
    kv_middle = exchange(outgoing(chunk_grids[1]))
    out_first, dq_first, mixed_first, own_grads = attend(
        kpos_rel, queries, douts, kv_first, factor, offsets[0], split,
        outgoing(chunk_grids[2]), mp_count,
    )
    kv_middle, mixed_first = lax.optimization_barrier((kv_middle, mixed_first))
    kv_last = exchange(mixed_first)
    out_middle, dq_middle, grads_middle = attend(
        kpos_rel, queries, douts, kv_middle, factor, offsets[1]
    )
    back_middle = exchange(grads_middle)
    own_row = jnp.arange(ctx_count, dtype=jnp.int32)[:, None] == my_stretch
    picker_others = jnp.where(own_row, jnp.zeros_like(picker_low), picker_low)
    first_rows = kv_last.reshape((ctx_count, mp_count) + kv_last.shape[1:])
    first_main = lax.dot_general(
        picker_others, first_rows, (((0,), (0,)), ((), ())), preferred_element_type=jnp.float32
    )
    middle_sum = absorb(back_middle)
    own_grads, first_main, middle_sum = lax.optimization_barrier(
        (own_grads, first_main, middle_sum)
    )
    gathered = lax.all_gather(own_grads, "mp", axis=0, tiled=True)
    gathered = gathered.reshape((mp_count, mp_count) + own_grads.shape[1:])
    own_back = lax.dynamic_index_in_dim(gathered, my_mp, 1, keepdims=False)
    own_pick = lax.dynamic_index_in_dim(picker_low, my_stretch, 0, keepdims=False)
    own_pick = own_pick.astype(jnp.float32).reshape(per_owner, 1, 1, 1, 1)
    first_sum = first_main + own_pick * own_back.astype(jnp.float32)[None]
    out_last, dq_last, grads_last = attend(
        kpos_rel, queries, douts, kv_last, factor, offsets[2]
    )
    back_last = exchange(grads_last)
    last_rows = back_last.reshape((ctx_count, mp_count) + back_last.shape[1:]).astype(jnp.float32)
    last_sum = jnp.stack([
        jnp.sum(jnp.where(picker[:, block_id].reshape(ctx_count, 1, 1, 1, 1), last_rows, 0.0), axis=0)
        for block_id in range(per_owner)
    ])
    summed = jnp.concatenate([first_sum, middle_sum, last_sum], axis=-1)
    summed = summed.transpose(2, 0, 3, 1, 4).reshape(2, kv_rows, full_width)
    attended = jnp.concatenate([out_first, out_middle, out_last], axis=-1)
    d_query = jnp.concatenate([dq_first, dq_middle, dq_last], axis=-1)
    return (attended, d_query, summed[0], summed[1])


def solution(mesh):
    return jax.shard_map(
        on_device,
        mesh=mesh,
        in_specs=(
            P(None, "ctx", "mp"),
            P(("ctx", "mp"), None),
            P(("ctx", "mp"), None),
            P(None, "ctx", "mp"),
            P("ctx", None),
        ),
        out_specs=(
            P(None, "ctx", "mp"),
            P(None, "ctx", "mp"),
            P(("ctx", "mp"), None),
            P(("ctx", "mp"), None),
        ),
        check_vma=False,
    )
```

```python
import functools
import math

import jax
import jax.numpy as jnp
from jax import lax
from jax.experimental import pallas as pl
from jax.experimental.pallas import tpu as pltpu
from jax.sharding import PartitionSpec as P

HD = 128
BLK = 16

neg_big = -1e30
far_pos = 1 << 30


def exchange(operand):
    return lax.all_to_all(operand, ("ctx", "mp"), split_axis=0, concat_axis=0, tiled=True)


def attend_kernel(*refs, factor, layer_count, mixed):
    if mixed:
        split_ref, kpos_ref, q_ref, do_ref, kv_ref, next_ref = refs[:6]
        o_ref, dq_ref, dkv_ref, own_ref, dk_acc, dv_acc = refs[6:]
    else:
        kpos_ref, q_ref, do_ref, kv_ref = refs[:4]
        o_ref, dq_ref, dkv_ref, dk_acc, dv_acc = refs[4:]
    layer_id = pl.program_id(1)
    q = q_ref[0]
    do = do_ref[0]
    key_total = dk_acc.shape[0]
    k = kv_ref[:, 0].reshape(key_total, HD)
    v = kv_ref[:, 1].reshape(key_total, HD)
    tok_rows = q.shape[0]
    rows = lax.broadcasted_iota(jnp.int32, (tok_rows, 1), 0)
    visible = kpos_ref[...] <= rows
    scores = lax.dot_general(
        q, k, (((1,), (1,)), ((), ())), preferred_element_type=jnp.float32
    ) * factor
    scores = jnp.where(visible, scores, neg_big)
    row_top = jnp.max(scores, axis=1, keepdims=True)
    raised = jnp.exp(scores - row_top)
    row_total = jnp.sum(raised, axis=1, keepdims=True)
    probs = raised * (1.0 / row_total)
    probs_low = probs.astype(jnp.bfloat16)
    attended = jnp.dot(probs_low, v, preferred_element_type=jnp.float32).astype(jnp.bfloat16)
    o_ref[0] = attended
    row_delta = jnp.sum(
        do.astype(jnp.float32) * attended.astype(jnp.float32), axis=1, keepdims=True
    )
    d_probs = lax.dot_general(
        do, v, (((1,), (1,)), ((), ())), preferred_element_type=jnp.float32
    )
    d_scores = (probs * (d_probs - row_delta)).astype(jnp.bfloat16)
    dq = jnp.dot(d_scores, k, preferred_element_type=jnp.float32) * factor
    dq_ref[0] = dq.astype(jnp.bfloat16)
    dk = lax.dot_general(
        d_scores, q, (((0,), (0,)), ((), ())), preferred_element_type=jnp.float32
    ) * factor
    dv = lax.dot_general(
        probs_low, do, (((0,), (0,)), ((), ())), preferred_element_type=jnp.float32
    )

    @pl.when(layer_id == 0)
    def _():
        dk_acc[...] = dk
        dv_acc[...] = dv

    @pl.when(layer_id > 0)
    def _():
        dk_acc[...] += dk
        dv_acc[...] += dv

    @pl.when(layer_id == layer_count - 1)
    def _():
        slot_count = dkv_ref.shape[0]
        dk_low = dk_acc[...].astype(jnp.bfloat16).reshape(slot_count, BLK, HD)
        dv_low = dv_acc[...].astype(jnp.bfloat16).reshape(slot_count, BLK, HD)
        if mixed:
            own_count = own_ref.shape[0]
            start_row = pl.multiple_of(split_ref[0] * BLK, own_count * BLK)
            own_k = dk_acc[pl.ds(start_row, own_count * BLK), :].astype(jnp.bfloat16)
            own_v = dv_acc[pl.ds(start_row, own_count * BLK), :].astype(jnp.bfloat16)
            own_ref[:, 0] = own_k.reshape(own_count, BLK, HD)
            own_ref[:, 1] = own_v.reshape(own_count, BLK, HD)
            slot_ids = lax.broadcasted_iota(jnp.int32, (slot_count, BLK, HD), 0)
            later = slot_ids >= split_ref[0]
            dk_low = jnp.where(later, next_ref[:, 0], dk_low)
            dv_low = jnp.where(later, next_ref[:, 1], dv_low)
        dkv_ref[:, 0] = dk_low
        dkv_ref[:, 1] = dv_low


def attend(
    kpos_rel, queries, douts, kv_rows, factor, head_offset, split=None, next_rows=None,
    own_slots=None,
):
    layer_count, tok_rows, _ = queries.shape
    slot_count, _, _, chunk_width = kv_rows.shape
    key_total = slot_count * BLK
    head_count = chunk_width // HD
    mixed = next_rows is not None
    kernel = functools.partial(
        attend_kernel, factor=factor, layer_count=layer_count, mixed=mixed
    )
    tok_in = pl.BlockSpec((1, tok_rows, HD), lambda h, l: (l, 0, h + head_offset))
    tok_out = pl.BlockSpec((1, tok_rows, HD), lambda h, l: (l, 0, h))
    kv_spec = pl.BlockSpec((slot_count, 2, BLK, HD), lambda h, l: (0, 0, 0, h))
    tok_shape = (layer_count, tok_rows, chunk_width)
    in_specs = [pl.BlockSpec((1, key_total), lambda h, l: (0, 0)), tok_in, tok_in, kv_spec]
    operands = [kpos_rel, queries, douts, kv_rows]
    out_specs = [tok_out, tok_out, kv_spec]
    out_shape = [
        jax.ShapeDtypeStruct(tok_shape, jnp.bfloat16),
        jax.ShapeDtypeStruct(tok_shape, jnp.bfloat16),
        jax.ShapeDtypeStruct(kv_rows.shape, jnp.bfloat16),
    ]
    if mixed:
        in_specs = [pl.BlockSpec(memory_space=pltpu.SMEM)] + in_specs + [kv_spec]
        operands = [split] + operands + [next_rows]
        own_count = own_slots
        out_specs.append(pl.BlockSpec((own_count, 2, BLK, HD), lambda h, l: (0, 0, 0, h)))
        out_shape.append(jax.ShapeDtypeStruct((own_count, 2, BLK, chunk_width), jnp.bfloat16))
    return pl.pallas_call(
        kernel,
        grid=(head_count, layer_count),
        in_specs=in_specs,
        out_specs=out_specs,
        out_shape=out_shape,
        scratch_shapes=[
            pltpu.VMEM((key_total, HD), jnp.float32),
            pltpu.VMEM((key_total, HD), jnp.float32),
        ],
        compiler_params=pltpu.CompilerParams(
            dimension_semantics=("arbitrary", "arbitrary"),
            vmem_limit_bytes=48 * 1024 * 1024,
        ),
    )(*operands)


def on_device(queries, cache_keys, cache_values, douts, reads):
    layer_count, tok_rows, head_width = queries.shape
    kv_rows, full_width = cache_keys.shape
    ctx_count = lax.axis_size("ctx")
    mp_count = lax.axis_size("mp")
    owner_count = ctx_count * mp_count
    per_owner = kv_rows // BLK
    my_owner = lax.axis_index(("ctx", "mp"))
    my_stretch = lax.axis_index("ctx")
    my_mp = lax.axis_index("mp")
    factor = 1.0 / math.sqrt(HD)
    spread = jnp.broadcast_to(reads, (owner_count, reads.shape[1]))
    all_lists = exchange(spread).reshape(ctx_count, mp_count, -1)[:, 0, :]
    owner_hit = (all_lists >= 0) & (all_lists // per_owner == my_owner)
    chosen = jnp.sum(jnp.where(owner_hit, all_lists - my_owner * per_owner, 0), axis=1)
    wanted = jnp.any(owner_hit, axis=1)
    picker = (chosen[:, None] == jnp.arange(per_owner, dtype=jnp.int32)[None, :]) & wanted[:, None]
    picker_low = picker.astype(jnp.bfloat16)

    def by_block(cache_rows):
        return cache_rows.reshape(per_owner, BLK, mp_count, head_width).transpose(0, 2, 1, 3)

    block_grid = jnp.stack([by_block(cache_keys), by_block(cache_values)], axis=2)
    head_count = head_width // HD
    outer_width = (2 * head_count // 5) * HD
    bounds = (0, outer_width, head_width - outer_width, head_width)
    chunk_grids = [block_grid[..., bounds[i]:bounds[i + 1]] for i in range(3)]

    def outgoing(chunk_grid):
        picked = jnp.zeros((ctx_count,) + chunk_grid.shape[1:], jnp.bfloat16)
        for block_id in range(per_owner):
            hit = picker[:, block_id].reshape(ctx_count, 1, 1, 1, 1)
            picked = jnp.where(hit, chunk_grid[block_id][None], picked)
        return picked.reshape((owner_count,) + chunk_grid.shape[2:])

    def absorb(returned):
        block_grid = returned.reshape((ctx_count, mp_count) + returned.shape[1:])
        return lax.dot_general(
            picker_low, block_grid, (((0,), (0,)), ((), ())), preferred_element_type=jnp.float32
        )

    own_list = reads[0]
    owner_ids = jnp.arange(owner_count, dtype=jnp.int32)
    slot_hit = (own_list[:, None] >= 0) & (own_list[:, None] // per_owner == owner_ids[None, :])
    slot_live = jnp.any(slot_hit, axis=0)
    slot_block = jnp.sum(
        jnp.where(slot_hit, own_list[:, None] - owner_ids[None, :] * per_owner, 0), axis=0
    )
    slot_start = owner_ids * kv_rows + slot_block * BLK
    key_pos = (slot_start[:, None] + jnp.arange(BLK, dtype=jnp.int32)[None, :]).reshape(-1)
    key_live = jnp.repeat(slot_live, BLK)
    kpos_rel = jnp.where(key_live, key_pos - my_stretch * tok_rows, far_pos)
    kpos_rel = kpos_rel.reshape(1, -1).astype(jnp.int32)
    split = (my_stretch * mp_count).reshape(1).astype(jnp.int32)
    offsets = [bound // HD for bound in bounds]
    kv_first = exchange(outgoing(chunk_grids[0]))
    kv_middle = exchange(outgoing(chunk_grids[1]))
    out_first, dq_first, mixed_first, own_grads = attend(
        kpos_rel, queries, douts, kv_first, factor, offsets[0], split,
        outgoing(chunk_grids[2]), mp_count,
    )
    kv_middle, mixed_first = lax.optimization_barrier((kv_middle, mixed_first))
    kv_last = exchange(mixed_first)
    out_middle, dq_middle, grads_middle = attend(
        kpos_rel, queries, douts, kv_middle, factor, offsets[1]
    )
    back_middle = exchange(grads_middle)
    own_row = jnp.arange(ctx_count, dtype=jnp.int32)[:, None] == my_stretch
    picker_others = jnp.where(own_row, jnp.zeros_like(picker_low), picker_low)
    first_rows = kv_last.reshape((ctx_count, mp_count) + kv_last.shape[1:])
    first_main = lax.dot_general(
        picker_others, first_rows, (((0,), (0,)), ((), ())), preferred_element_type=jnp.float32
    )
    middle_sum = absorb(back_middle)
    own_grads, first_main, middle_sum = lax.optimization_barrier(
        (own_grads, first_main, middle_sum)
    )
    gathered = lax.all_gather(own_grads, "mp", axis=0, tiled=True)
    gathered = gathered.reshape((mp_count, mp_count) + own_grads.shape[1:])
    own_back = lax.dynamic_index_in_dim(gathered, my_mp, 1, keepdims=False)
    own_pick = lax.dynamic_index_in_dim(picker_low, my_stretch, 0, keepdims=False)
    own_pick = own_pick.astype(jnp.float32).reshape(per_owner, 1, 1, 1, 1)
    first_sum = first_main + own_pick * own_back.astype(jnp.float32)[None]
    out_last, dq_last, grads_last = attend(
        kpos_rel, queries, douts, kv_last, factor, offsets[2]
    )
    back_last = exchange(grads_last)
    early = [part.transpose(2, 0, 3, 1, 4) for part in (first_sum, middle_sum)]
    early = lax.optimization_barrier(early)
    late = absorb(back_last).transpose(2, 0, 3, 1, 4)
    summed = jnp.concatenate(early + [late], axis=-1).reshape(2, kv_rows, full_width)
    attended = jnp.concatenate([out_first, out_middle, out_last], axis=-1)
    d_query = jnp.concatenate([dq_first, dq_middle, dq_last], axis=-1)
    return (attended, d_query, summed[0], summed[1])


def solution(mesh):
    return jax.shard_map(
        on_device,
        mesh=mesh,
        in_specs=(
            P(None, "ctx", "mp"),
            P(("ctx", "mp"), None),
            P(("ctx", "mp"), None),
            P(None, "ctx", "mp"),
            P("ctx", None),
        ),
        out_specs=(
            P(None, "ctx", "mp"),
            P(None, "ctx", "mp"),
            P(("ctx", "mp"), None),
            P(("ctx", "mp"), None),
        ),
        check_vma=False,
    )
```

```python
import functools
import math

import jax
import jax.numpy as jnp
from jax import lax
from jax.experimental import pallas as pl
from jax.experimental.pallas import tpu as pltpu
from jax.sharding import PartitionSpec as P

HD = 128
BLK = 16

neg_big = -1e30
far_pos = 1 << 30


def exchange(operand):
    return lax.all_to_all(operand, ("ctx", "mp"), split_axis=0, concat_axis=0, tiled=True)


def attend_kernel(*refs, factor, layer_count, mixed):
    if mixed:
        split_ref, kpos_ref, q_ref, do_ref, kv_ref, next_ref = refs[:6]
        o_ref, dq_ref, dkv_ref, own_ref, dk_acc, dv_acc = refs[6:]
    else:
        kpos_ref, q_ref, do_ref, kv_ref = refs[:4]
        o_ref, dq_ref, dkv_ref, dk_acc, dv_acc = refs[4:]
    layer_id = pl.program_id(1)
    q = q_ref[0]
    do = do_ref[0]
    key_total = dk_acc.shape[0]
    k = kv_ref[:, 0].reshape(key_total, HD)
    v = kv_ref[:, 1].reshape(key_total, HD)
    tok_rows = q.shape[0]
    rows = lax.broadcasted_iota(jnp.int32, (tok_rows, 1), 0)
    visible = kpos_ref[...] <= rows
    scores = lax.dot_general(
        q, k, (((1,), (1,)), ((), ())), preferred_element_type=jnp.float32
    ) * factor
    scores = jnp.where(visible, scores, neg_big)
    row_top = jnp.max(scores, axis=1, keepdims=True)
    raised = jnp.exp(scores - row_top)
    row_total = jnp.sum(raised, axis=1, keepdims=True)
    probs = raised * (1.0 / row_total)
    probs_low = probs.astype(jnp.bfloat16)
    attended = jnp.dot(probs_low, v, preferred_element_type=jnp.float32).astype(jnp.bfloat16)
    o_ref[0] = attended
    row_delta = jnp.sum(
        do.astype(jnp.float32) * attended.astype(jnp.float32), axis=1, keepdims=True
    )
    d_probs = lax.dot_general(
        do, v, (((1,), (1,)), ((), ())), preferred_element_type=jnp.float32
    )
    d_scores = (probs * (d_probs - row_delta)).astype(jnp.bfloat16)
    dq = jnp.dot(d_scores, k, preferred_element_type=jnp.float32) * factor
    dq_ref[0] = dq.astype(jnp.bfloat16)
    dk = lax.dot_general(
        d_scores, q, (((0,), (0,)), ((), ())), preferred_element_type=jnp.float32
    ) * factor
    dv = lax.dot_general(
        probs_low, do, (((0,), (0,)), ((), ())), preferred_element_type=jnp.float32
    )

    @pl.when(layer_id == 0)
    def _():
        dk_acc[...] = dk
        dv_acc[...] = dv

    @pl.when(layer_id > 0)
    def _():
        dk_acc[...] += dk
        dv_acc[...] += dv

    @pl.when(layer_id == layer_count - 1)
    def _():
        slot_count = dkv_ref.shape[0]
        dk_low = dk_acc[...].astype(jnp.bfloat16).reshape(slot_count, BLK, HD)
        dv_low = dv_acc[...].astype(jnp.bfloat16).reshape(slot_count, BLK, HD)
        if mixed:
            own_count = own_ref.shape[0]
            start_row = pl.multiple_of(split_ref[0] * BLK, own_count * BLK)
            own_k = dk_acc[pl.ds(start_row, own_count * BLK), :].astype(jnp.bfloat16)
            own_v = dv_acc[pl.ds(start_row, own_count * BLK), :].astype(jnp.bfloat16)
            own_ref[:, 0] = own_k.reshape(own_count, BLK, HD)
            own_ref[:, 1] = own_v.reshape(own_count, BLK, HD)
            slot_ids = lax.broadcasted_iota(jnp.int32, (slot_count, BLK, HD), 0)
            later = slot_ids >= split_ref[0]
            dk_low = jnp.where(later, next_ref[:, 0], dk_low)
            dv_low = jnp.where(later, next_ref[:, 1], dv_low)
        dkv_ref[:, 0] = dk_low
        dkv_ref[:, 1] = dv_low


def attend(
    kpos_rel, queries, douts, kv_rows, factor, head_offset, split=None, next_rows=None,
    own_slots=None,
):
    layer_count, tok_rows, _ = queries.shape
    slot_count, _, _, chunk_width = kv_rows.shape
    key_total = slot_count * BLK
    head_count = chunk_width // HD
    mixed = next_rows is not None
    kernel = functools.partial(
        attend_kernel, factor=factor, layer_count=layer_count, mixed=mixed
    )
    tok_in = pl.BlockSpec((1, tok_rows, HD), lambda h, l: (l, 0, h + head_offset))
    tok_out = pl.BlockSpec((1, tok_rows, HD), lambda h, l: (l, 0, h))
    kv_spec = pl.BlockSpec((slot_count, 2, BLK, HD), lambda h, l: (0, 0, 0, h))
    tok_shape = (layer_count, tok_rows, chunk_width)
    in_specs = [pl.BlockSpec((1, key_total), lambda h, l: (0, 0)), tok_in, tok_in, kv_spec]
    operands = [kpos_rel, queries, douts, kv_rows]
    out_specs = [tok_out, tok_out, kv_spec]
    out_shape = [
        jax.ShapeDtypeStruct(tok_shape, jnp.bfloat16),
        jax.ShapeDtypeStruct(tok_shape, jnp.bfloat16),
        jax.ShapeDtypeStruct(kv_rows.shape, jnp.bfloat16),
    ]
    if mixed:
        in_specs = [pl.BlockSpec(memory_space=pltpu.SMEM)] + in_specs + [kv_spec]
        operands = [split] + operands + [next_rows]
        own_count = own_slots
        out_specs.append(pl.BlockSpec((own_count, 2, BLK, HD), lambda h, l: (0, 0, 0, h)))
        out_shape.append(jax.ShapeDtypeStruct((own_count, 2, BLK, chunk_width), jnp.bfloat16))
    return pl.pallas_call(
        kernel,
        grid=(head_count, layer_count),
        in_specs=in_specs,
        out_specs=out_specs,
        out_shape=out_shape,
        scratch_shapes=[
            pltpu.VMEM((key_total, HD), jnp.float32),
            pltpu.VMEM((key_total, HD), jnp.float32),
        ],
        compiler_params=pltpu.CompilerParams(
            dimension_semantics=("arbitrary", "arbitrary"),
            vmem_limit_bytes=48 * 1024 * 1024,
        ),
    )(*operands)


def on_device(queries, cache_keys, cache_values, douts, reads):
    layer_count, tok_rows, head_width = queries.shape
    kv_rows, full_width = cache_keys.shape
    ctx_count = lax.axis_size("ctx")
    mp_count = lax.axis_size("mp")
    owner_count = ctx_count * mp_count
    per_owner = kv_rows // BLK
    my_owner = lax.axis_index(("ctx", "mp"))
    my_stretch = lax.axis_index("ctx")
    my_mp = lax.axis_index("mp")
    factor = 1.0 / math.sqrt(HD)
    spread = jnp.broadcast_to(reads, (ctx_count, reads.shape[1]))
    all_lists = lax.all_to_all(spread, "ctx", split_axis=0, concat_axis=0, tiled=True)
    owner_hit = (all_lists >= 0) & (all_lists // per_owner == my_owner)
    chosen = jnp.sum(jnp.where(owner_hit, all_lists - my_owner * per_owner, 0), axis=1)
    wanted = jnp.any(owner_hit, axis=1)
    picker = (chosen[:, None] == jnp.arange(per_owner, dtype=jnp.int32)[None, :]) & wanted[:, None]
    picker_low = picker.astype(jnp.bfloat16)

    def by_block(cache_rows):
        return cache_rows.reshape(per_owner, BLK, mp_count, head_width).transpose(0, 2, 1, 3)

    block_grid = jnp.stack([by_block(cache_keys), by_block(cache_values)], axis=2)
    head_count = head_width // HD
    outer_width = (2 * head_count // 5) * HD
    bounds = (0, outer_width, head_width - outer_width, head_width)
    chunk_grids = [block_grid[..., bounds[i]:bounds[i + 1]] for i in range(3)]

    def outgoing(chunk_grid):
        picked = jnp.zeros((ctx_count,) + chunk_grid.shape[1:], jnp.bfloat16)
        for block_id in range(per_owner):
            hit = picker[:, block_id].reshape(ctx_count, 1, 1, 1, 1)
            picked = jnp.where(hit, chunk_grid[block_id][None], picked)
        return picked.reshape((owner_count,) + chunk_grid.shape[2:])

    def absorb(returned):
        block_grid = returned.reshape((ctx_count, mp_count) + returned.shape[1:])
        return lax.dot_general(
            picker_low, block_grid, (((0,), (0,)), ((), ())), preferred_element_type=jnp.float32
        )

    own_list = reads[0]
    owner_ids = jnp.arange(owner_count, dtype=jnp.int32)
    slot_hit = (own_list[:, None] >= 0) & (own_list[:, None] // per_owner == owner_ids[None, :])
    slot_live = jnp.any(slot_hit, axis=0)
    slot_block = jnp.sum(
        jnp.where(slot_hit, own_list[:, None] - owner_ids[None, :] * per_owner, 0), axis=0
    )
    slot_start = owner_ids * kv_rows + slot_block * BLK
    key_pos = (slot_start[:, None] + jnp.arange(BLK, dtype=jnp.int32)[None, :]).reshape(-1)
    key_live = jnp.repeat(slot_live, BLK)
    kpos_rel = jnp.where(key_live, key_pos - my_stretch * tok_rows, far_pos)
    kpos_rel = kpos_rel.reshape(1, -1).astype(jnp.int32)
    split = (my_stretch * mp_count).reshape(1).astype(jnp.int32)
    offsets = [bound // HD for bound in bounds]
    kv_first = exchange(outgoing(chunk_grids[0]))
    kv_middle = exchange(outgoing(chunk_grids[1]))
    out_first, dq_first, mixed_first, own_grads = attend(
        kpos_rel, queries, douts, kv_first, factor, offsets[0], split,
        outgoing(chunk_grids[2]), mp_count,
    )
    kv_middle, mixed_first = lax.optimization_barrier((kv_middle, mixed_first))
    kv_last = exchange(mixed_first)
    out_middle, dq_middle, grads_middle = attend(
        kpos_rel, queries, douts, kv_middle, factor, offsets[1]
    )
    back_middle = exchange(grads_middle)
    own_row = jnp.arange(ctx_count, dtype=jnp.int32)[:, None] == my_stretch
    picker_others = jnp.where(own_row, jnp.zeros_like(picker_low), picker_low)
    first_rows = kv_last.reshape((ctx_count, mp_count) + kv_last.shape[1:])
    first_main = lax.dot_general(
        picker_others, first_rows, (((0,), (0,)), ((), ())), preferred_element_type=jnp.float32
    )
    middle_sum = absorb(back_middle)
    own_grads, first_main, middle_sum = lax.optimization_barrier(
        (own_grads, first_main, middle_sum)
    )
    gathered = lax.all_gather(own_grads, "mp", axis=0, tiled=True)
    gathered = gathered.reshape((mp_count, mp_count) + own_grads.shape[1:])
    own_back = lax.dynamic_index_in_dim(gathered, my_mp, 1, keepdims=False)
    own_pick = lax.dynamic_index_in_dim(picker_low, my_stretch, 0, keepdims=False)
    own_pick = own_pick.astype(jnp.float32).reshape(per_owner, 1, 1, 1, 1)
    first_sum = first_main + own_pick * own_back.astype(jnp.float32)[None]
    out_last, dq_last, grads_last = attend(
        kpos_rel, queries, douts, kv_last, factor, offsets[2]
    )
    back_last = exchange(grads_last)
    summed = jnp.concatenate([first_sum, middle_sum, absorb(back_last)], axis=-1)
    summed = summed.transpose(2, 0, 3, 1, 4).reshape(2, kv_rows, full_width)
    attended = jnp.concatenate([out_first, out_middle, out_last], axis=-1)
    d_query = jnp.concatenate([dq_first, dq_middle, dq_last], axis=-1)
    return (attended, d_query, summed[0], summed[1])


def solution(mesh):
    return jax.shard_map(
        on_device,
        mesh=mesh,
        in_specs=(
            P(None, "ctx", "mp"),
            P(("ctx", "mp"), None),
            P(("ctx", "mp"), None),
            P(None, "ctx", "mp"),
            P("ctx", None),
        ),
        out_specs=(
            P(None, "ctx", "mp"),
            P(None, "ctx", "mp"),
            P(("ctx", "mp"), None),
            P(("ctx", "mp"), None),
        ),
        check_vma=False,
    )
```
